128 devices in a mesh: section: 4 (over x_hi, core), dom: 32 (over z, y, x_lo).
Axes of the slice: x: 4 (x_hi: 2, x_lo: 2; x = x_hi * 2 + x_lo), y: 4, z: 4, core: 2. Of those that a mesh axis runs over, the one named last changes fastest.
Arguments:
- features: bfloat16 [4, 4096, 512], P(None, 'dom'), may hold values from -6 to 6
- adjacency: bfloat16 [4, 64, 64, 2112], P(None, 'dom'), may hold values from -0.125 to 0.125
- boundary: int32 [4, 32, 32], replicated, may hold values from 0 to 1
- layer_counts: int32 [4], P('section'), may hold values from 0 to 2, as said below
- weights: bfloat16 [4, 2, 512, 512], P('section'), may hold values from -0.25 to 0.25
Outputs:
- stashed: bfloat16 [4, 4, 4096, 512], P('section', None, 'dom')
The draws below stay inside these ranges and needn't reach their ends.
Inputs may be any that keep to these rules, and one draw needn't show every extreme that they name: `layer_counts`: the number of layer slots that section uses; some section uses all 2 and some none. `boundary`: a local block index within the sending partition.
All inputs are finite; a program needn't handle non-finite values.
Results may differ from the reference program's by a relative error of at most 0.009.
Values may be sent and summed in bfloat16 or wider, within the bound.
No kernel may reach another device: no remote copies, remote signals or barrier semaphores. Data moves between devices by JAX's collectives and lax.ppermute only.
A program may use at most 64 MiB of HBM per device.

```python
import jax
import jax.numpy as jnp
from jax import lax

D = 512
BLOCK = 64
CAP = 2
NB = 2
MICRO = 4
SLOTS = 33
NODES = 4096
ALL_BLOCKS = 64
N_SECTION = 4
N_DOM = 32


def draw_layer_counts(key, part):
    base = jax.random.randint(key, (N_SECTION,), 0, CAP + 1)
    where_full = jax.random.randint(jax.random.fold_in(key, 1), (), 0, N_SECTION)
    offset = jax.random.randint(jax.random.fold_in(key, 2), (), 1, N_SECTION)
    where_empty = (where_full + offset) % N_SECTION
    position = jnp.arange(N_SECTION)
    base = jnp.where(position == where_full, CAP, base)
    base = jnp.where(position == where_empty, 0, base)
    return base.astype(jnp.int32)


def with_ends(array, key, least, largest):
    dims = array.shape
    spot = [jax.random.randint(jax.random.fold_in(key, axis), (), 0, dims[axis]) for axis in range(len(dims))]
    array = array.at[tuple(spot)].set(least)
    longest = dims.index(max(dims))
    spot[longest] = (spot[longest] + 1) % dims[longest]
    return array.at[tuple(spot)].set(largest)


def steps_of(own_key, dims, cuts, smallest, high):
    factor_of = 1.0
    for dim, blocks in cuts:
        heights = jax.random.uniform(jax.random.fold_in(jax.random.fold_in(own_key, 6), dim), (blocks,), jnp.float32, smallest / len(cuts), high / len(cuts))
        factor_of = factor_of * jnp.repeat(jnp.exp(heights), dims[dim] // blocks).reshape((-1,) + (1,) * (len(dims) - 1 - dim))
    return factor_of


def centred(key, dims, scale, most, pieces=(), kind=jnp.bfloat16):
    loudness = steps_of(key, dims, pieces, -0.22, 0.18) if pieces else 1.0
    result = jax.random.normal(key, dims, jnp.float32) * scale * loudness
    return jnp.minimum(jnp.maximum(result, -most), most).astype(kind)


def setup_inputs(seed: int = 0) -> dict:
    key_list = jax.random.split(jax.random.key(seed), 6)
    return {
        "features": centred(key_list[0], (MICRO, NODES, D), 1.0, 6.0, ((1, 32),)),
        "adjacency": centred(key_list[1], (MICRO, ALL_BLOCKS, BLOCK, SLOTS * BLOCK), (SLOTS * BLOCK) ** -0.5, 0.125, ((1, 32),)),
        "boundary": with_ends(jax.random.randint(key_list[2], (MICRO, N_DOM, N_DOM), 0, NB), jax.random.fold_in(key_list[2], 1), 0, NB - 1).astype(jnp.int32),
        "layer_counts": draw_layer_counts(jax.random.fold_in(key_list[5], 71), 0),
        "weights": centred(key_list[4], (N_SECTION, CAP, D, D), D ** -0.5, 0.25, ((0, 4),)),
    }


def apply_layer(hidden, adj_tiles, bound_ids, weight):
    blocks = hidden.reshape(N_DOM, NB, BLOCK, D)
    senders = jnp.arange(N_DOM, dtype=jnp.int32)
    outbound = blocks[senders[:, None], bound_ids]
    source_part = (senders[:, None] + 1 + jnp.arange(N_DOM - 1, dtype=jnp.int32)[None, :]) % N_DOM
    incoming = outbound[source_part, senders[:, None]]
    sources = jnp.concatenate([blocks, incoming], axis=1).reshape(N_DOM, SLOTS * BLOCK, D)
    tiles = adj_tiles.reshape(N_DOM, NB * BLOCK, SLOTS * BLOCK)
    aggregate = jnp.einsum('pik,pkd->pid', tiles.astype(jnp.float32), sources.astype(jnp.float32))
    aggregate = aggregate.reshape(NODES, D)
    mean_square = lax.optimization_barrier(jnp.mean(aggregate * aggregate, axis=-1, keepdims=True))
    normed = (aggregate * lax.rsqrt(mean_square + 1e-06)).astype(jnp.bfloat16)
    projected = jnp.dot(normed, weight, preferred_element_type=jnp.float32)
    return (hidden.astype(jnp.float32) + jax.nn.relu(projected)).astype(jnp.bfloat16)

def reference(features, adjacency, boundary, layer_counts, weights):
    batched = jax.vmap(apply_layer, in_axes=(0, 0, 0, None))

    def section_step(hidden, inputs):
        section_weights, count = inputs
        for slot in range(CAP):
            updated = batched(hidden, adjacency, boundary, section_weights[slot])
            hidden = jnp.where(slot < count, updated, hidden)
        return (hidden, hidden)
    final_state, stashed = lax.scan(section_step, features, (weights, layer_counts))
    return stashed
```

```python
import jax
import jax.numpy as jnp
from jax import lax
from jax.sharding import PartitionSpec as P


def shifted(value, axis, steps):
    count = lax.axis_size(axis)
    return lax.ppermute(value, axis, [(source, (source + steps) % count) for source in range(count)])


def local(features, adjacency, boundary, layer_counts, weights):
    section_count = lax.axis_size("section")
    part_count = lax.axis_size("dom")
    group = lax.axis_index("section")
    part_here = lax.axis_index("dom")
    local_rows = features.shape[1]
    feature_width = features.shape[2]
    local_blocks = adjacency.shape[1]
    block_rows = adjacency.shape[2]
    slot_total = weights.shape[1]

    section_weights_shifted = [weights[0]]
    counts_shifted = [layer_counts]
    for step in range(1, section_count):
        section_weights_shifted.append(shifted(weights[0], "section", step))
        counts_shifted.append(shifted(layer_counts, "section", step))
    weight_stack = jnp.stack(section_weights_shifted)
    count_stack = jnp.concatenate(counts_shifted)
    inverse = (group - jnp.arange(section_count, dtype=jnp.int32)) % section_count
    count_by_section = count_stack[inverse]

    hidden = lax.dynamic_index_in_dim(features, group, 0, keepdims=False)
    adj_tiles = lax.dynamic_index_in_dim(adjacency, group, 0, keepdims=False)
    bound_ids = lax.dynamic_index_in_dim(boundary, group, 0, keepdims=False)
    send_ids = [bound_ids[part_here, (part_here - step) % part_count] for step in range(1, part_count)]

    def apply_layer(hidden, weight):
        local_view = hidden.reshape(local_blocks, block_rows, feature_width)
        incoming = [
            shifted(local_view[send_ids[step - 1]], "dom", -step) for step in range(1, part_count)
        ]
        sources = jnp.concatenate([local_view, jnp.stack(incoming)], axis=0)
        sources = sources.reshape(-1, feature_width)
        aggregate = jnp.einsum(
            "bik,kd->bid", adj_tiles, sources, preferred_element_type=jnp.float32
        )
        aggregate = aggregate.reshape(local_rows, feature_width)
        mean_square = jnp.mean(aggregate * aggregate, axis=-1, keepdims=True)
        normed = (aggregate * lax.rsqrt(mean_square + 1e-06)).astype(jnp.bfloat16)
        projected = jnp.dot(normed, weight, preferred_element_type=jnp.float32)
        return (hidden.astype(jnp.float32) + jax.nn.relu(projected)).astype(jnp.bfloat16)

    stash = []
    for section in range(section_count):
        shift_of = (group - section) % section_count
        weight_here = lax.dynamic_index_in_dim(weight_stack, shift_of, 0, keepdims=False)
        count_here = count_by_section[section]
        for slot in range(slot_total):
            hidden = lax.cond(
                slot < count_here,
                lambda h, w=weight_here[slot]: apply_layer(h, w),
                lambda h: h,
                hidden,
            )
        stash.append(hidden)

    gathered = []
    for step in range(section_count):
        piece = jnp.stack(stash)[(group + step) % section_count]
        gathered.append(piece if step == 0 else shifted(piece, "section", step))
    gathered = jnp.stack(gathered)
    micro_order = (group - jnp.arange(section_count, dtype=jnp.int32)) % section_count
    out = gathered[micro_order]
    return out[None]


def solution(mesh):
    in_specs = (
        P(None, "dom", None),
        P(None, "dom", None, None),
        P(),
        P("section"),
        P("section", None, None, None),
    )
    out_specs = P("section", None, "dom", None)
    return jax.shard_map(local, mesh=mesh, in_specs=in_specs, out_specs=out_specs, check_vma=False)
```

```python
import jax
import jax.numpy as jnp
from jax import lax
from jax.sharding import PartitionSpec as P


def shifted(value, axis, steps):
    count = lax.axis_size(axis)
    return lax.ppermute(value, axis, [(source, (source + steps) % count) for source in range(count)])


def sent_one_way(value, axis, source, target):
    return lax.ppermute(value, axis, [(source, target)])


def local(features, adjacency, boundary, layer_counts, weights):
    section_count = lax.axis_size("section")
    part_count = lax.axis_size("dom")
    group = lax.axis_index("section")
    part_here = lax.axis_index("dom")
    local_rows = features.shape[1]
    feature_width = features.shape[2]
    local_blocks = adjacency.shape[1]
    block_rows = adjacency.shape[2]
    slot_total = weights.shape[1]

    counts_shifted = [layer_counts] + [
        shifted(layer_counts, "section", step) for step in range(1, section_count)
    ]
    count_stack = jnp.concatenate(counts_shifted)
    count_by_section = count_stack[(group - jnp.arange(section_count, dtype=jnp.int32)) % section_count]
    trips = jnp.clip(count_by_section, 0, slot_total)

    weight_by_section = []
    for section in range(section_count):
        received = weights[0]
        for target in range(section_count):
            if target != section:
                piece = sent_one_way(weights[0], "section", section, target)
                received = jnp.where(group == target, piece, received)
        weight_by_section.append(received)

    hidden = lax.dynamic_index_in_dim(features, group, 0, keepdims=False)
    adj_tiles = lax.dynamic_index_in_dim(adjacency, group, 0, keepdims=False)
    bound_ids = lax.dynamic_index_in_dim(boundary, group, 0, keepdims=False)
    send_ids = bound_ids[part_here]
    local_cols = local_blocks * block_rows
    adj_local = adj_tiles[:, :, :local_cols]
    adj_remote = adj_tiles[:, :, local_cols:].reshape(local_blocks, block_rows, part_count - 1, block_rows)
    adj_remote = jnp.concatenate(
        [adj_remote, jnp.zeros((local_blocks, block_rows, 1, block_rows), adj_remote.dtype)], axis=2
    )
    slot_of_part = (jnp.arange(part_count, dtype=jnp.int32) - part_here - 1) % part_count
    adj_by_part = adj_remote[:, :, slot_of_part, :].reshape(local_blocks, block_rows, part_count * block_rows)
    adj_ordered = jnp.concatenate([adj_local, adj_by_part], axis=2)

    def apply_layer(hidden, weight):
        local_view = hidden.reshape(local_blocks, block_rows, feature_width)
        outgoing = local_view[send_ids]
        incoming = lax.all_to_all(outgoing, "dom", 0, 0, tiled=True)
        sources = jnp.concatenate([local_view, incoming], axis=0)
        sources = sources.reshape(-1, feature_width)
        aggregate = jnp.einsum(
            "bik,kd->bid", adj_ordered, sources, preferred_element_type=jnp.float32
        )
        aggregate = aggregate.reshape(local_rows, feature_width)
        mean_square = jnp.mean(aggregate * aggregate, axis=-1, keepdims=True)
        normed = (aggregate * lax.rsqrt(mean_square + 1e-06)).astype(jnp.bfloat16)
        projected = jnp.dot(normed, weight, preferred_element_type=jnp.float32)
        return (hidden.astype(jnp.float32) + jax.nn.relu(projected)).astype(jnp.bfloat16)

    stash = []
    for section in range(section_count):
        section_weight = weight_by_section[section]
        hidden = lax.fori_loop(
            0,
            trips[section],
            lambda slot, h, w=section_weight: apply_layer(
                h, lax.dynamic_index_in_dim(w, slot, 0, keepdims=False)
            ),
            hidden,
        )
        stash.append(hidden)

    by_micro = []
    for micro in range(section_count):
        received = stash[micro]
        for section in range(section_count):
            if section != micro:
                piece = sent_one_way(stash[section], "section", micro, section)
                received = jnp.where(group == section, piece, received)
        by_micro.append(received)
    out = jnp.stack(by_micro)
    return out[None]


def solution(mesh):
    in_specs = (
        P(None, "dom", None),
        P(None, "dom", None, None),
        P(),
        P("section"),
        P("section", None, None, None),
    )
    out_specs = P("section", None, "dom", None)
    return jax.shard_map(local, mesh=mesh, in_specs=in_specs, out_specs=out_specs, check_vma=False)
```

```python
import jax
import jax.numpy as jnp
from jax import lax
from jax.sharding import PartitionSpec as P


def shifted(value, axis, steps):
    count = lax.axis_size(axis)
    return lax.ppermute(value, axis, [(source, (source + steps) % count) for source in range(count)])


def sent_one_way(value, axis, source, target):
    return lax.ppermute(value, axis, [(source, target)])


def local(features, adjacency, boundary, layer_counts, weights):
    section_count = lax.axis_size("section")
    part_count = lax.axis_size("dom")
    group = lax.axis_index("section")
    part_here = lax.axis_index("dom")
    local_rows = features.shape[1]
    feature_width = features.shape[2]
    local_blocks = adjacency.shape[1]
    block_rows = adjacency.shape[2]
    slot_total = weights.shape[1]

    counts_shifted = [layer_counts] + [
        shifted(layer_counts, "section", step) for step in range(1, section_count)
    ]
    count_stack = jnp.concatenate(counts_shifted)
    count_by_section = count_stack[(group - jnp.arange(section_count, dtype=jnp.int32)) % section_count]
    trips = jnp.clip(count_by_section, 0, slot_total)

    hidden = lax.dynamic_index_in_dim(features, group, 0, keepdims=False)
    adj_tiles = lax.dynamic_index_in_dim(adjacency, group, 0, keepdims=False)
    bound_ids = lax.dynamic_index_in_dim(boundary, group, 0, keepdims=False)
    send_ids = bound_ids[part_here]
    local_cols = local_blocks * block_rows
    adj_local = adj_tiles[:, :, :local_cols]
    adj_remote = adj_tiles[:, :, local_cols:].reshape(local_blocks, block_rows, part_count - 1, block_rows)
    adj_remote = jnp.concatenate(
        [adj_remote, jnp.zeros((local_blocks, block_rows, 1, block_rows), adj_remote.dtype)], axis=2
    )
    slot_of_part = (jnp.arange(part_count, dtype=jnp.int32) - part_here - 1) % part_count
    adj_by_part = adj_remote[:, :, slot_of_part, :].reshape(local_blocks, block_rows, part_count * block_rows)
    adj_ordered = jnp.concatenate([adj_local, adj_by_part], axis=2)

    def apply_layer(hidden, weight):
        local_view = hidden.reshape(local_blocks, block_rows, feature_width)
        outgoing = local_view[send_ids]
        incoming = lax.all_to_all(outgoing, "dom", 0, 0, tiled=True)
        sources = jnp.concatenate([local_view, incoming], axis=0)
        sources = sources.reshape(-1, feature_width)
        aggregate = jnp.einsum(
            "bik,kd->bid", adj_ordered, sources, preferred_element_type=jnp.float32
        )
        aggregate = aggregate.reshape(local_rows, feature_width)
        mean_square = jnp.mean(aggregate * aggregate, axis=-1, keepdims=True)
        normed = (aggregate * lax.rsqrt(mean_square + 1e-06)).astype(jnp.bfloat16)
        projected = jnp.dot(normed, weight, preferred_element_type=jnp.float32)
        return (hidden.astype(jnp.float32) + jax.nn.relu(projected)).astype(jnp.bfloat16)

    def weight_of(section, slot):
        own = lax.dynamic_index_in_dim(weights[0], slot, 0, keepdims=False)
        received = own
        for target in range(section_count):
            if target != section:
                piece = sent_one_way(own, "section", section, target)
                received = jnp.where(group == target, piece, received)
        return received

    stash = []
    for section in range(section_count):
        hidden = lax.fori_loop(
            0,
            trips[section],
            lambda slot, h, s=section: apply_layer(h, weight_of(s, slot)),
            hidden,
        )
        stash.append(hidden)

    stash_stack = jnp.stack(stash)
    arrived = [lax.dynamic_index_in_dim(stash_stack, group, 0, keepdims=False)]
    for step in range(1, section_count):
        piece = lax.dynamic_index_in_dim(stash_stack, (group + step) % section_count, 0, keepdims=False)
        arrived.append(shifted(piece, "section", step))
    arrived = jnp.stack(arrived)
    out = arrived[(group - jnp.arange(section_count, dtype=jnp.int32)) % section_count]
    return out[None]


def solution(mesh):
    in_specs = (
        P(None, "dom", None),
        P(None, "dom", None, None),
        P(),
        P("section"),
        P("section", None, None, None),
    )
    out_specs = P("section", None, "dom", None)
    return jax.shard_map(local, mesh=mesh, in_specs=in_specs, out_specs=out_specs, check_vma=False)
```

```python
import jax
import jax.numpy as jnp
from jax import lax
from jax.sharding import PartitionSpec as P


def shifted(value, axis, steps):
    count = lax.axis_size(axis)
    return lax.ppermute(value, axis, [(source, (source + steps) % count) for source in range(count)])


def sent_one_way(value, axis, source, target):
    return lax.ppermute(value, axis, [(source, target)])


def local(features, adjacency, boundary, layer_counts, weights):
    section_count = lax.axis_size("section")
    part_count = lax.axis_size("dom")
    group = lax.axis_index("section")
    part_here = lax.axis_index("dom")
    local_rows = features.shape[1]
    feature_width = features.shape[2]
    local_blocks = adjacency.shape[1]
    block_rows = adjacency.shape[2]
    slot_total = weights.shape[1]

    counts_shifted = [layer_counts] + [
        shifted(layer_counts, "section", step) for step in range(1, section_count)
    ]
    count_stack = jnp.concatenate(counts_shifted)
    count_by_section = count_stack[(group - jnp.arange(section_count, dtype=jnp.int32)) % section_count]
    trips = jnp.clip(count_by_section, 0, slot_total)

    hidden = lax.dynamic_index_in_dim(features, group, 0, keepdims=False)
    adj_tiles = lax.dynamic_index_in_dim(adjacency, group, 0, keepdims=False)
    bound_ids = lax.dynamic_index_in_dim(boundary, group, 0, keepdims=False)
    send_ids = bound_ids[part_here]
    source_order = (part_here + 1 + jnp.arange(part_count - 1, dtype=jnp.int32)) % part_count

    def apply_layer(hidden, weight):
        local_view = hidden.reshape(local_blocks, block_rows, feature_width)
        outgoing = local_view[send_ids]
        incoming = lax.all_to_all(outgoing, "dom", 0, 0, tiled=True)
        sources = jnp.concatenate([local_view, incoming[source_order]], axis=0)
        sources = sources.reshape(-1, feature_width)
        aggregate = jnp.einsum(
            "bik,kd->bid", adj_tiles, sources, preferred_element_type=jnp.float32
        )
        aggregate = aggregate.reshape(local_rows, feature_width)
        mean_square = jnp.mean(aggregate * aggregate, axis=-1, keepdims=True)
        normed = (aggregate * lax.rsqrt(mean_square + 1e-06)).astype(jnp.bfloat16)
        projected = jnp.dot(normed, weight, preferred_element_type=jnp.float32)
        return (hidden.astype(jnp.float32) + jax.nn.relu(projected)).astype(jnp.bfloat16)

    def weight_of(section, slot):
        own = lax.dynamic_index_in_dim(weights[0], slot, 0, keepdims=False)
        received = own
        for target in range(section_count):
            if target != section:
                piece = sent_one_way(own, "section", section, target)
                received = jnp.where(group == target, piece, received)
        return received

    stash = []
    for section in range(section_count):
        hidden = lax.fori_loop(
            0,
            trips[section],
            lambda slot, h, s=section: apply_layer(h, weight_of(s, slot)),
            hidden,
        )
        stash.append(hidden)

    stash_stack = jnp.stack(stash)
    arrived = [lax.dynamic_index_in_dim(stash_stack, group, 0, keepdims=False)]
    for step in range(1, section_count):
        piece = lax.dynamic_index_in_dim(stash_stack, (group + step) % section_count, 0, keepdims=False)
        arrived.append(shifted(piece, "section", step))
    arrived = jnp.stack(arrived)
    out = arrived[(group - jnp.arange(section_count, dtype=jnp.int32)) % section_count]
    return out[None]


def solution(mesh):
    in_specs = (
        P(None, "dom", None),
        P(None, "dom", None, None),
        P(),
        P("section"),
        P("section", None, None, None),
    )
    out_specs = P("section", None, "dom", None)
    return jax.shard_map(local, mesh=mesh, in_specs=in_specs, out_specs=out_specs, check_vma=False)
```

```python
import jax
import jax.numpy as jnp
from jax import lax
from jax.sharding import PartitionSpec as P


def shifted(value, axis, steps):
    count = lax.axis_size(axis)
    return lax.ppermute(value, axis, [(source, (source + steps) % count) for source in range(count)])


def sent_one_way(value, axis, source, target):
    return lax.ppermute(value, axis, [(source, target)])


def local(features, adjacency, boundary, layer_counts, weights):
    section_count = lax.axis_size("section")
    part_count = lax.axis_size("dom")
    group = lax.axis_index("section")
    part_here = lax.axis_index("dom")
    local_rows = features.shape[1]
    feature_width = features.shape[2]
    local_blocks = adjacency.shape[1]
    block_rows = adjacency.shape[2]
    slot_total = weights.shape[1]

    counts_shifted = [layer_counts] + [
        shifted(layer_counts, "section", step) for step in range(1, section_count)
    ]
    count_stack = jnp.concatenate(counts_shifted)
    count_by_section = count_stack[(group - jnp.arange(section_count, dtype=jnp.int32)) % section_count]
    trips = jnp.clip(count_by_section, 0, slot_total)

    hidden = lax.dynamic_index_in_dim(features, group, 0, keepdims=False)
    adj_tiles = lax.dynamic_index_in_dim(adjacency, group, 0, keepdims=False)
    bound_ids = lax.dynamic_index_in_dim(boundary, group, 0, keepdims=False)
    send_ids = bound_ids[part_here]
    source_order = (part_here + 1 + jnp.arange(part_count - 1, dtype=jnp.int32)) % part_count

    def apply_layer(hidden, weight):
        local_view = hidden.reshape(local_blocks, block_rows, feature_width)
        outgoing = local_view[send_ids]
        incoming = lax.all_to_all(outgoing, "dom", 0, 0, tiled=True)
        sources = jnp.concatenate([local_view, incoming[source_order]], axis=0)
        sources = sources.reshape(-1, feature_width)
        aggregate = jnp.einsum(
            "bik,kd->bid", adj_tiles, sources, preferred_element_type=jnp.float32
        )
        aggregate = aggregate.reshape(local_rows, feature_width)
        mean_square = jnp.mean(aggregate * aggregate, axis=-1, keepdims=True)
        normed = (aggregate * lax.rsqrt(mean_square + 1e-06)).astype(jnp.bfloat16)
        projected = jnp.dot(normed, weight, preferred_element_type=jnp.float32)
        return (hidden.astype(jnp.float32) + jax.nn.relu(projected)).astype(jnp.bfloat16)

    def weight_of(section, slot):
        own = lax.dynamic_index_in_dim(weights[0], slot, 0, keepdims=False)
        if section_count != 4:
            received = own
            for target in range(section_count):
                if target != section:
                    piece = sent_one_way(own, "section", section, target)
                    received = jnp.where(group == target, piece, received)
            return received
        far = section ^ 2
        across = sent_one_way(own, "section", section, far)
        held = jnp.where(group == far, across, own)
        beside = lax.ppermute(held, "section", [(section, section ^ 1), (far, far ^ 1)])
        return jnp.where((group == section) | (group == far), held, beside)

    stash = []
    for section in range(section_count):
        hidden = lax.fori_loop(
            0,
            trips[section],
            lambda slot, h, s=section: apply_layer(h, weight_of(s, slot)),
            hidden,
        )
        stash.append(hidden)

    stash_stack = jnp.stack(stash)
    arrived = [lax.dynamic_index_in_dim(stash_stack, group, 0, keepdims=False)]
    for step in range(1, section_count):
        piece = lax.dynamic_index_in_dim(stash_stack, (group + step) % section_count, 0, keepdims=False)
        arrived.append(shifted(piece, "section", step))
    arrived = jnp.stack(arrived)
    out = arrived[(group - jnp.arange(section_count, dtype=jnp.int32)) % section_count]
    return out[None]


def solution(mesh):
    in_specs = (
        P(None, "dom", None),
        P(None, "dom", None, None),
        P(),
        P("section"),
        P("section", None, None, None),
    )
    out_specs = P("section", None, "dom", None)
    return jax.shard_map(local, mesh=mesh, in_specs=in_specs, out_specs=out_specs, check_vma=False)
```

```python
import jax
import jax.numpy as jnp
from jax import lax
from jax.sharding import PartitionSpec as P


def shifted(value, axis, steps):
    count = lax.axis_size(axis)
    return lax.ppermute(value, axis, [(source, (source + steps) % count) for source in range(count)])


def sent_one_way(value, axis, source, target):
    return lax.ppermute(value, axis, [(source, target)])


def local(features, adjacency, boundary, layer_counts, weights):
    section_count = lax.axis_size("section")
    part_count = lax.axis_size("dom")
    group = lax.axis_index("section")
    part_here = lax.axis_index("dom")
    local_rows = features.shape[1]
    feature_width = features.shape[2]
    local_blocks = adjacency.shape[1]
    block_rows = adjacency.shape[2]
    slot_total = weights.shape[1]

    counts_shifted = [layer_counts] + [
        shifted(layer_counts, "section", step) for step in range(1, section_count)
    ]
    count_stack = jnp.concatenate(counts_shifted)
    count_by_section = count_stack[(group - jnp.arange(section_count, dtype=jnp.int32)) % section_count]
    trips = jnp.clip(count_by_section, 0, slot_total)

    hidden = lax.dynamic_index_in_dim(features, group, 0, keepdims=False)
    adj_tiles = lax.dynamic_index_in_dim(adjacency, group, 0, keepdims=False)
    bound_ids = lax.dynamic_index_in_dim(boundary, group, 0, keepdims=False)
    send_ids = bound_ids[part_here]
    source_order = (part_here + 1 + jnp.arange(part_count - 1, dtype=jnp.int32)) % part_count

    def normed_of(hidden):
        local_view = hidden.reshape(local_blocks, block_rows, feature_width)
        outgoing = local_view[send_ids]
        incoming = lax.all_to_all(outgoing, "dom", 0, 0, tiled=True)
        sources = jnp.concatenate([local_view, incoming[source_order]], axis=0)
        sources = sources.reshape(-1, feature_width)
        aggregate = jnp.einsum(
            "bik,kd->bid", adj_tiles, sources, preferred_element_type=jnp.float32
        )
        aggregate = aggregate.reshape(local_rows, feature_width)
        mean_square = jnp.mean(aggregate * aggregate, axis=-1, keepdims=True)
        return (aggregate * lax.rsqrt(mean_square + 1e-06)).astype(jnp.bfloat16)

    def projected_onto(hidden, normed, weight):
        projected = jnp.dot(normed, weight, preferred_element_type=jnp.float32)
        return (hidden.astype(jnp.float32) + jax.nn.relu(projected)).astype(jnp.bfloat16)

    if section_count == 4:
        across = shifted(weights[0], "section", 2)
        beside = lax.ppermute(
            jnp.stack([weights[0], across]), "section", [(0, 1), (1, 0), (2, 3), (3, 2)]
        )
        weight_list = jnp.stack([weights[0], beside[0], across, beside[1]])

        def list_index(section):
            return jnp.bitwise_xor(section, group)
    else:
        weight_list = jnp.stack(
            [weights[0]] + [shifted(weights[0], "section", step) for step in range(1, section_count)]
        )

        def list_index(section):
            return (group - section) % section_count

    finished = jnp.cumsum(trips)
    total = finished[-1]

    def weight_for(layer):
        section = jnp.sum((finished <= layer).astype(jnp.int32))
        section = jnp.minimum(section, section_count - 1)
        slot = layer - (finished[section] - trips[section])
        slot = jnp.clip(slot, 0, slot_total - 1)
        chosen = lax.dynamic_index_in_dim(weight_list, list_index(section), 0, keepdims=False)
        return lax.dynamic_index_in_dim(chosen, slot, 0, keepdims=False)

    def recorded(stash, hidden, done):
        return jnp.where((finished == done)[:, None, None], hidden[None], stash)

    stash = jnp.broadcast_to(hidden[None], (section_count,) + hidden.shape)
    normed = normed_of(hidden)

    def layer_step(layer, carry):
        hidden, normed, stash = carry
        hidden = projected_onto(hidden, normed, weight_for(layer))
        stash = recorded(stash, hidden, layer + 1)
        return hidden, normed_of(hidden), stash

    hidden, normed, stash = lax.fori_loop(
        0, jnp.maximum(total - 1, 0), layer_step, (hidden, normed, stash)
    )
    last = jnp.maximum(total - 1, 0)
    hidden = projected_onto(hidden, normed, weight_for(last))
    stash = jnp.where(total >= 1, recorded(stash, hidden, total), stash)

    stash_stack = stash
    arrived = [lax.dynamic_index_in_dim(stash_stack, group, 0, keepdims=False)]
    for step in range(1, section_count):
        piece = lax.dynamic_index_in_dim(stash_stack, (group + step) % section_count, 0, keepdims=False)
        arrived.append(shifted(piece, "section", step))
    arrived = jnp.stack(arrived)
    out = arrived[(group - jnp.arange(section_count, dtype=jnp.int32)) % section_count]
    return out[None]


def solution(mesh):
    in_specs = (
        P(None, "dom", None),
        P(None, "dom", None, None),
        P(),
        P("section"),
        P("section", None, None, None),
    )
    out_specs = P("section", None, "dom", None)
    return jax.shard_map(local, mesh=mesh, in_specs=in_specs, out_specs=out_specs, check_vma=False)
```

```python
import jax
import jax.numpy as jnp
from jax import lax
from jax.sharding import PartitionSpec as P


def shifted(value, axis, steps):
    count = lax.axis_size(axis)
    return lax.ppermute(value, axis, [(source, (source + steps) % count) for source in range(count)])


def sent_one_way(value, axis, source, target):
    return lax.ppermute(value, axis, [(source, target)])


def local(features, adjacency, boundary, layer_counts, weights):
    section_count = lax.axis_size("section")
    part_count = lax.axis_size("dom")
    group = lax.axis_index("section")
    part_here = lax.axis_index("dom")
    local_rows = features.shape[1]
    feature_width = features.shape[2]
    local_blocks = adjacency.shape[1]
    block_rows = adjacency.shape[2]
    slot_total = weights.shape[1]

    counts_shifted = [layer_counts] + [
        shifted(layer_counts, "section", step) for step in range(1, section_count)
    ]
    count_stack = jnp.concatenate(counts_shifted)
    count_by_section = count_stack[(group - jnp.arange(section_count, dtype=jnp.int32)) % section_count]
    trips = jnp.clip(count_by_section, 0, slot_total)

    hidden = lax.dynamic_index_in_dim(features, group, 0, keepdims=False)
    adj_tiles = lax.dynamic_index_in_dim(adjacency, group, 0, keepdims=False)
    bound_ids = lax.dynamic_index_in_dim(boundary, group, 0, keepdims=False)
    send_ids = bound_ids[part_here]
    local_cols = local_blocks * block_rows
    adj_t = adj_tiles.reshape(local_cols, -1).T.reshape(-1, block_rows, local_cols)
    adj_t_local = adj_t[:local_blocks].reshape(local_cols, local_cols)
    adj_t_remote = jnp.concatenate(
        [adj_t[local_blocks:], jnp.zeros((1, block_rows, local_cols), adj_t.dtype)], axis=0
    )
    slot_of_part = (jnp.arange(part_count, dtype=jnp.int32) - part_here - 1) % part_count
    adj_t_by_part = adj_t_remote[slot_of_part].reshape(part_count * block_rows, local_cols)

    def normed_of(hidden):
        local_view = hidden.reshape(local_blocks, block_rows, feature_width)
        outgoing = local_view[send_ids]
        incoming = lax.all_to_all(outgoing, "dom", 0, 0, tiled=True)
        aggregate = jnp.einsum(
            "kb,kd->bd", adj_t_local, hidden, preferred_element_type=jnp.float32
        ) + jnp.einsum(
            "kb,kd->bd", adj_t_by_part, incoming.reshape(-1, feature_width),
            preferred_element_type=jnp.float32,
        )
        mean_square = jnp.mean(aggregate * aggregate, axis=-1, keepdims=True)
        return (aggregate * lax.rsqrt(mean_square + 1e-06)).astype(jnp.bfloat16)

    def projected_onto(hidden, normed, weight):
        projected = jnp.dot(normed, weight, preferred_element_type=jnp.float32)
        return (hidden.astype(jnp.float32) + jax.nn.relu(projected)).astype(jnp.bfloat16)

    if section_count == 4:
        across = shifted(weights[0], "section", 2)
        beside = lax.ppermute(
            jnp.stack([weights[0], across]), "section", [(0, 1), (1, 0), (2, 3), (3, 2)]
        )
        weight_list = jnp.stack([weights[0], beside[0], across, beside[1]])

        def list_index(section):
            return jnp.bitwise_xor(section, group)
    else:
        weight_list = jnp.stack(
            [weights[0]] + [shifted(weights[0], "section", step) for step in range(1, section_count)]
        )

        def list_index(section):
            return (group - section) % section_count

    finished = jnp.cumsum(trips)
    total = finished[-1]

    def weight_for(layer):
        section = jnp.sum((finished <= layer).astype(jnp.int32))
        section = jnp.minimum(section, section_count - 1)
        slot = layer - (finished[section] - trips[section])
        slot = jnp.clip(slot, 0, slot_total - 1)
        chosen = lax.dynamic_index_in_dim(weight_list, list_index(section), 0, keepdims=False)
        return lax.dynamic_index_in_dim(chosen, slot, 0, keepdims=False)

    def recorded(stash, hidden, done):
        return jnp.where((finished == done)[:, None, None], hidden[None], stash)

    stash = jnp.broadcast_to(hidden[None], (section_count,) + hidden.shape)
    normed = normed_of(hidden)

    def layer_step(layer, carry):
        hidden, normed, stash = carry
        hidden = projected_onto(hidden, normed, weight_for(layer))
        stash = recorded(stash, hidden, layer + 1)
        return hidden, normed_of(hidden), stash

    hidden, normed, stash = lax.fori_loop(
        0, jnp.maximum(total - 1, 0), layer_step, (hidden, normed, stash)
    )
    last = jnp.maximum(total - 1, 0)
    hidden = projected_onto(hidden, normed, weight_for(last))
    stash = jnp.where(total >= 1, recorded(stash, hidden, total), stash)

    stash_stack = stash
    arrived = [lax.dynamic_index_in_dim(stash_stack, group, 0, keepdims=False)]
    for step in range(1, section_count):
        piece = lax.dynamic_index_in_dim(stash_stack, (group + step) % section_count, 0, keepdims=False)
        arrived.append(shifted(piece, "section", step))
    arrived = jnp.stack(arrived)
    out = arrived[(group - jnp.arange(section_count, dtype=jnp.int32)) % section_count]
    return out[None]


def solution(mesh):
    in_specs = (
        P(None, "dom", None),
        P(None, "dom", None, None),
        P(),
        P("section"),
        P("section", None, None, None),
    )
    out_specs = P("section", None, "dom", None)
    return jax.shard_map(local, mesh=mesh, in_specs=in_specs, out_specs=out_specs, check_vma=False)
```

```python
import jax
import jax.numpy as jnp
from jax import lax
from jax.sharding import PartitionSpec as P


def shifted(value, axis, steps):
    count = lax.axis_size(axis)
    return lax.ppermute(value, axis, [(source, (source + steps) % count) for source in range(count)])


def sent_one_way(value, axis, source, target):
    return lax.ppermute(value, axis, [(source, target)])


def local(features, adjacency, boundary, layer_counts, weights):
    section_count = lax.axis_size("section")
    part_count = lax.axis_size("dom")
    group = lax.axis_index("section")
    part_here = lax.axis_index("dom")
    local_rows = features.shape[1]
    feature_width = features.shape[2]
    local_blocks = adjacency.shape[1]
    block_rows = adjacency.shape[2]
    slot_total = weights.shape[1]

    counts_shifted = [layer_counts] + [
        shifted(layer_counts, "section", step) for step in range(1, section_count)
    ]
    count_stack = jnp.concatenate(counts_shifted)
    count_by_section = count_stack[(group - jnp.arange(section_count, dtype=jnp.int32)) % section_count]
    trips = jnp.clip(count_by_section, 0, slot_total)

    hidden = lax.dynamic_index_in_dim(features, group, 0, keepdims=False)
    adj_tiles = lax.dynamic_index_in_dim(adjacency, group, 0, keepdims=False)
    bound_ids = lax.dynamic_index_in_dim(boundary, group, 0, keepdims=False)
    send_ids = bound_ids[part_here]
    local_cols = local_blocks * block_rows
    adj_t = adj_tiles.reshape(local_cols, -1).T.reshape(-1, block_rows, local_cols)
    adj_t_local = adj_t[:local_blocks].reshape(local_cols, local_cols)
    adj_t_remote = jnp.concatenate(
        [adj_t[local_blocks:], jnp.zeros((1, block_rows, local_cols), adj_t.dtype)], axis=0
    )
    slot_of_part = (jnp.arange(part_count, dtype=jnp.int32) - part_here - 1) % part_count
    adj_t_by_part = adj_t_remote[slot_of_part].reshape(part_count * block_rows, local_cols)

    def normed_of(hidden):
        local_view = hidden.reshape(local_blocks, block_rows, feature_width)
        outgoing = local_view[send_ids]
        incoming = lax.all_to_all(outgoing, "dom", 0, 0, tiled=True)
        aggregate = jnp.einsum(
            "kb,kd->bd", adj_t_local, hidden, preferred_element_type=jnp.float32
        ) + jnp.einsum(
            "kb,kd->bd", adj_t_by_part, incoming.reshape(-1, feature_width),
            preferred_element_type=jnp.float32,
        )
        mean_square = jnp.mean(aggregate * aggregate, axis=-1, keepdims=True)
        return (aggregate * lax.rsqrt(mean_square + 1e-06)).astype(jnp.bfloat16)

    def projected_onto(hidden, normed, weight):
        projected = jnp.dot(normed, weight, preferred_element_type=jnp.float32)
        return (hidden.astype(jnp.float32) + jax.nn.relu(projected)).astype(jnp.bfloat16)

    if section_count == 4 and part_count % 2 == 0:
        pairs = [
            (section * part_count + part, (section ^ 2) * part_count + (part ^ 1))
            for section in range(section_count)
            for part in range(part_count)
        ]
        across = lax.ppermute(weights[0], ("section", "dom"), pairs)
        core_swap = [(0, 1), (1, 0), (2, 3), (3, 2)]
        beside_own = lax.ppermute(weights[0], "section", core_swap)
        beside_far = lax.ppermute(across, "section", core_swap)
        weight_list = jnp.stack([weights[0], beside_own, across, beside_far])

        def list_index(section):
            return jnp.bitwise_xor(section, group)
    else:
        weight_list = jnp.stack(
            [weights[0]] + [shifted(weights[0], "section", step) for step in range(1, section_count)]
        )

        def list_index(section):
            return (group - section) % section_count

    finished = jnp.cumsum(trips)
    total = finished[-1]

    def weight_for(layer):
        section = jnp.sum((finished <= layer).astype(jnp.int32))
        section = jnp.minimum(section, section_count - 1)
        slot = layer - (finished[section] - trips[section])
        slot = jnp.clip(slot, 0, slot_total - 1)
        chosen = lax.dynamic_index_in_dim(weight_list, list_index(section), 0, keepdims=False)
        return lax.dynamic_index_in_dim(chosen, slot, 0, keepdims=False)

    def recorded(stash, hidden, done):
        return jnp.where((finished == done)[:, None, None], hidden[None], stash)

    stash = jnp.broadcast_to(hidden[None], (section_count,) + hidden.shape)
    normed = normed_of(hidden)

    def layer_step(layer, carry):
        hidden, normed, stash = carry
        hidden = projected_onto(hidden, normed, weight_for(layer))
        stash = recorded(stash, hidden, layer + 1)
        return hidden, normed_of(hidden), stash

    hidden, normed, stash = lax.fori_loop(
        0, jnp.maximum(total - 1, 0), layer_step, (hidden, normed, stash)
    )
    last = jnp.maximum(total - 1, 0)
    hidden = projected_onto(hidden, normed, weight_for(last))
    stash = jnp.where(total >= 1, recorded(stash, hidden, total), stash)

    stash_stack = stash
    arrived = [lax.dynamic_index_in_dim(stash_stack, group, 0, keepdims=False)]
    for step in range(1, section_count):
        piece = lax.dynamic_index_in_dim(stash_stack, (group + step) % section_count, 0, keepdims=False)
        arrived.append(shifted(piece, "section", step))
    arrived = jnp.stack(arrived)
    out = arrived[(group - jnp.arange(section_count, dtype=jnp.int32)) % section_count]
    return out[None]


def solution(mesh):
    in_specs = (
        P(None, "dom", None),
        P(None, "dom", None, None),
        P(),
        P("section"),
        P("section", None, None, None),
    )
    out_specs = P("section", None, "dom", None)
    return jax.shard_map(local, mesh=mesh, in_specs=in_specs, out_specs=out_specs, check_vma=False)
```

```python
import jax
import jax.numpy as jnp
from jax import lax
from jax.sharding import PartitionSpec as P


def shifted(value, axis, steps):
    count = lax.axis_size(axis)
    return lax.ppermute(value, axis, [(source, (source + steps) % count) for source in range(count)])


def sent_one_way(value, axis, source, target):
    return lax.ppermute(value, axis, [(source, target)])


def local(features, adjacency, boundary, layer_counts, weights):
    section_count = lax.axis_size("section")
    part_count = lax.axis_size("dom")
    group = lax.axis_index("section")
    part_here = lax.axis_index("dom")
    local_rows = features.shape[1]
    feature_width = features.shape[2]
    local_blocks = adjacency.shape[1]
    block_rows = adjacency.shape[2]
    slot_total = weights.shape[1]

    hidden = lax.dynamic_index_in_dim(features, group, 0, keepdims=False)
    adj_tiles = lax.dynamic_index_in_dim(adjacency, group, 0, keepdims=False)
    bound_ids = lax.dynamic_index_in_dim(boundary, group, 0, keepdims=False)
    send_ids = bound_ids[part_here]
    local_cols = local_blocks * block_rows
    adj_t = adj_tiles.reshape(local_cols, -1).T.reshape(-1, block_rows, local_cols)
    adj_t_local = adj_t[:local_blocks].reshape(local_cols, local_cols)
    adj_t_remote = jnp.concatenate(
        [adj_t[local_blocks:], jnp.zeros((1, block_rows, local_cols), adj_t.dtype)], axis=0
    )
    slot_of_part = (jnp.arange(part_count, dtype=jnp.int32) - part_here - 1) % part_count
    adj_t_by_part = adj_t_remote[slot_of_part].reshape(part_count * block_rows, local_cols)

    def normed_of(hidden):
        local_view = hidden.reshape(local_blocks, block_rows, feature_width)
        outgoing = local_view[send_ids]
        incoming = lax.all_to_all(outgoing, "dom", 0, 0, tiled=True)
        aggregate = jnp.einsum(
            "kb,kd->bd", adj_t_local, hidden, preferred_element_type=jnp.float32
        ) + jnp.einsum(
            "kb,kd->bd", adj_t_by_part, incoming.reshape(-1, feature_width),
            preferred_element_type=jnp.float32,
        )
        mean_square = jnp.mean(aggregate * aggregate, axis=-1, keepdims=True)
        return (aggregate * lax.rsqrt(mean_square + 1e-06)).astype(jnp.bfloat16)

    def projected_onto(hidden, normed, weight):
        projected = jnp.dot(normed, weight, preferred_element_type=jnp.float32)
        return (hidden.astype(jnp.float32) + jax.nn.relu(projected)).astype(jnp.bfloat16)

    if section_count == 4 and part_count % 2 == 0:
        pairs = [
            (section * part_count + part, (section ^ 2) * part_count + (part ^ 1))
            for section in range(section_count)
            for part in range(part_count)
        ]
        core_swap = [(0, 1), (1, 0), (2, 3), (3, 2)]

        def spread(value):
            across = lax.ppermute(value, ("section", "dom"), pairs)
            beside_own = lax.ppermute(value, "section", core_swap)
            beside_far = lax.ppermute(across, "section", core_swap)
            return jnp.stack([value, beside_own, across, beside_far])

        def list_index(section):
            return jnp.bitwise_xor(section, group)
    else:
        def spread(value):
            return jnp.stack(
                [value] + [shifted(value, "section", step) for step in range(1, section_count)]
            )

        def list_index(section):
            return (group - section) % section_count

    count_list = spread(layer_counts)[:, 0]
    count_by_section = count_list[list_index(jnp.arange(section_count, dtype=jnp.int32))]
    trips = jnp.clip(count_by_section, 0, slot_total)
    weight_list = spread(weights[0]).reshape((section_count * slot_total,) + weights.shape[2:])

    finished = jnp.cumsum(trips)
    total = finished[-1]

    def weight_for(layer):
        section = jnp.sum((finished <= layer).astype(jnp.int32))
        section = jnp.minimum(section, section_count - 1)
        slot = layer - (finished[section] - trips[section])
        slot = jnp.clip(slot, 0, slot_total - 1)
        return lax.dynamic_index_in_dim(weight_list, list_index(section) * slot_total + slot, 0, keepdims=False)

    def recorded(stash, hidden, done):
        return jnp.where((finished == done)[:, None, None], hidden[None], stash)

    stash = jnp.broadcast_to(hidden[None], (section_count,) + hidden.shape)
    normed = normed_of(hidden)

    def layer_step(layer, carry):
        hidden, normed, stash = carry
        hidden = projected_onto(hidden, normed, weight_for(layer))
        stash = recorded(stash, hidden, layer + 1)
        return hidden, normed_of(hidden), stash

    hidden, normed, stash = lax.fori_loop(
        0, jnp.maximum(total - 1, 0), layer_step, (hidden, normed, stash)
    )
    last = jnp.maximum(total - 1, 0)
    hidden = projected_onto(hidden, normed, weight_for(last))
    stash = jnp.where(total >= 1, recorded(stash, hidden, total), stash)

    stash_stack = stash
    arrived = [lax.dynamic_index_in_dim(stash_stack, group, 0, keepdims=False)]
    for step in range(1, section_count):
        piece = lax.dynamic_index_in_dim(stash_stack, (group + step) % section_count, 0, keepdims=False)
        arrived.append(shifted(piece, "section", step))
    arrived = jnp.stack(arrived)
    out = arrived[(group - jnp.arange(section_count, dtype=jnp.int32)) % section_count]
    return out[None]


def solution(mesh):
    in_specs = (
        P(None, "dom", None),
        P(None, "dom", None, None),
        P(),
        P("section"),
        P("section", None, None, None),
    )
    out_specs = P("section", None, "dom", None)
    return jax.shard_map(local, mesh=mesh, in_specs=in_specs, out_specs=out_specs, check_vma=False)
```

```python
import jax
import jax.numpy as jnp
from jax import lax
from jax.sharding import PartitionSpec as P


def shifted(value, axis, steps):
    count = lax.axis_size(axis)
    return lax.ppermute(value, axis, [(source, (source + steps) % count) for source in range(count)])


def sent_one_way(value, axis, source, target):
    return lax.ppermute(value, axis, [(source, target)])


def local(features, adjacency, boundary, layer_counts, weights):
    section_count = lax.axis_size("section")
    part_count = lax.axis_size("dom")
    group = lax.axis_index("section")
    part_here = lax.axis_index("dom")
    local_rows = features.shape[1]
    feature_width = features.shape[2]
    local_blocks = adjacency.shape[1]
    block_rows = adjacency.shape[2]
    slot_total = weights.shape[1]

    hidden = lax.dynamic_index_in_dim(features, group, 0, keepdims=False)
    adj_tiles = lax.dynamic_index_in_dim(adjacency, group, 0, keepdims=False)
    bound_ids = lax.dynamic_index_in_dim(boundary, group, 0, keepdims=False)
    send_ids = bound_ids[part_here]
    local_cols = local_blocks * block_rows
    adj_t = adj_tiles.reshape(local_cols, -1).T.reshape(-1, block_rows, local_cols)
    adj_t_local = adj_t[:local_blocks].reshape(local_cols, local_cols)
    adj_t_remote = jnp.concatenate(
        [adj_t[local_blocks:], jnp.zeros((1, block_rows, local_cols), adj_t.dtype)], axis=0
    )
    slot_of_part = (jnp.arange(part_count, dtype=jnp.int32) - part_here - 1) % part_count
    adj_t_by_part = adj_t_remote[slot_of_part].reshape(part_count * block_rows, local_cols)

    def normed_of(hidden):
        local_view = hidden.reshape(local_blocks, block_rows, feature_width)
        outgoing = local_view[send_ids]
        incoming = lax.all_to_all(outgoing, "dom", 0, 0, tiled=True)
        aggregate = jnp.einsum(
            "kb,kd->bd", adj_t_local, hidden, preferred_element_type=jnp.float32
        ) + jnp.einsum(
            "kb,kd->bd", adj_t_by_part, incoming.reshape(-1, feature_width),
            preferred_element_type=jnp.float32,
        )
        mean_square = jnp.mean(aggregate * aggregate, axis=-1, keepdims=True)
        return (aggregate * lax.rsqrt(mean_square + 1e-06)).astype(jnp.bfloat16)

    def projected_onto(hidden, normed, weight):
        projected = jnp.dot(normed, weight, preferred_element_type=jnp.float32)
        return (hidden.astype(jnp.float32) + jax.nn.relu(projected)).astype(jnp.bfloat16)

    if section_count == 4 and part_count % 2 == 0:
        pairs = [
            (section * part_count + part, (section ^ 2) * part_count + (part ^ 1))
            for section in range(section_count)
            for part in range(part_count)
        ]
        core_swap = [(0, 1), (1, 0), (2, 3), (3, 2)]

        def spread(value):
            across = lax.ppermute(value, ("section", "dom"), pairs)
            beside_own = lax.ppermute(value, "section", core_swap)
            beside_far = lax.ppermute(across, "section", core_swap)
            return jnp.stack([value, beside_own, across, beside_far])

        def list_index(section):
            return jnp.bitwise_xor(section, group)
    else:
        def spread(value):
            return jnp.stack(
                [value] + [shifted(value, "section", step) for step in range(1, section_count)]
            )

        def list_index(section):
            return (group - section) % section_count

    count_list = spread(layer_counts)[:, 0]
    count_by_section = count_list[list_index(jnp.arange(section_count, dtype=jnp.int32))]
    trips = jnp.clip(count_by_section, 0, slot_total)
    weight_list = spread(weights[0]).reshape((section_count * slot_total,) + weights.shape[2:])

    finished = jnp.cumsum(trips)
    total = finished[-1]

    layers = jnp.arange(section_count * slot_total, dtype=jnp.int32)
    layer_section = jnp.sum((finished[None, :] <= layers[:, None]).astype(jnp.int32), axis=1)
    layer_section = jnp.minimum(layer_section, section_count - 1)
    layer_slot = layers - (finished[layer_section] - trips[layer_section])
    layer_slot = jnp.clip(layer_slot, 0, slot_total - 1)
    weight_row = list_index(layer_section) * slot_total + layer_slot

    def weight_for(layer):
        return lax.dynamic_index_in_dim(weight_list, weight_row[layer], 0, keepdims=False)

    def recorded(stash, hidden, done):
        return jnp.where((finished == done)[:, None, None], hidden[None], stash)

    stash = jnp.broadcast_to(hidden[None], (section_count,) + hidden.shape)
    normed = normed_of(hidden)

    def layer_step(layer, carry):
        hidden, normed, stash, weight = carry
        hidden = projected_onto(hidden, normed, weight)
        stash = recorded(stash, hidden, layer + 1)
        return hidden, normed_of(hidden), stash, weight_for(layer + 1)

    hidden, normed, stash, weight = lax.fori_loop(
        0, jnp.maximum(total - 1, 0), layer_step, (hidden, normed, stash, weight_for(0))
    )
    hidden = projected_onto(hidden, normed, weight)
    stash = jnp.where(total >= 1, recorded(stash, hidden, total), stash)

    stash_stack = stash
    arrived = [lax.dynamic_index_in_dim(stash_stack, group, 0, keepdims=False)]
    for step in range(1, section_count):
        piece = lax.dynamic_index_in_dim(stash_stack, (group + step) % section_count, 0, keepdims=False)
        arrived.append(shifted(piece, "section", step))
    arrived = jnp.stack(arrived)
    out = arrived[(group - jnp.arange(section_count, dtype=jnp.int32)) % section_count]
    return out[None]


def solution(mesh):
    in_specs = (
        P(None, "dom", None),
        P(None, "dom", None, None),
        P(),
        P("section"),
        P("section", None, None, None),
    )
    out_specs = P("section", None, "dom", None)
    return jax.shard_map(local, mesh=mesh, in_specs=in_specs, out_specs=out_specs, check_vma=False)
```

```python
import jax
import jax.numpy as jnp
from jax import lax
from jax.sharding import PartitionSpec as P


def shifted(value, axis, steps):
    count = lax.axis_size(axis)
    return lax.ppermute(value, axis, [(source, (source + steps) % count) for source in range(count)])


def sent_one_way(value, axis, source, target):
    return lax.ppermute(value, axis, [(source, target)])


def local(features, adjacency, boundary, layer_counts, weights):
    section_count = lax.axis_size("section")
    part_count = lax.axis_size("dom")
    group = lax.axis_index("section")
    part_here = lax.axis_index("dom")
    local_rows = features.shape[1]
    feature_width = features.shape[2]
    local_blocks = adjacency.shape[1]
    block_rows = adjacency.shape[2]
    slot_total = weights.shape[1]

    hidden = lax.dynamic_index_in_dim(features, group, 0, keepdims=False)
    adj_tiles = lax.dynamic_index_in_dim(adjacency, group, 0, keepdims=False)
    bound_ids = lax.dynamic_index_in_dim(boundary, group, 0, keepdims=False)
    send_ids = bound_ids[part_here]
    local_cols = local_blocks * block_rows
    adj_t = adj_tiles.reshape(local_cols, -1).T.reshape(-1, block_rows, local_cols)
    adj_t_local = adj_t[:local_blocks].reshape(local_cols, local_cols)
    adj_t_remote = jnp.concatenate(
        [adj_t[local_blocks:], jnp.zeros((1, block_rows, local_cols), adj_t.dtype)], axis=0
    )
    slot_of_part = (jnp.arange(part_count, dtype=jnp.int32) - part_here - 1) % part_count
    adj_t_by_part = adj_t_remote[slot_of_part].reshape(part_count * block_rows, local_cols)

    def normed_of(hidden):
        local_view = hidden.reshape(local_blocks, block_rows, feature_width)
        outgoing = local_view[send_ids]
        incoming = lax.all_to_all(outgoing, "dom", 0, 0, tiled=True)
        aggregate = jnp.einsum(
            "kb,kd->bd", adj_t_local, hidden, preferred_element_type=jnp.float32
        ) + jnp.einsum(
            "kb,kd->bd", adj_t_by_part, incoming.reshape(-1, feature_width),
            preferred_element_type=jnp.float32,
        )
        mean_square = jnp.mean(aggregate * aggregate, axis=-1, keepdims=True)
        return (aggregate * lax.rsqrt(mean_square + 1e-06)).astype(jnp.bfloat16)

    def projected_onto(hidden, normed, weight):
        projected = jnp.dot(normed, weight, preferred_element_type=jnp.float32)
        return (hidden.astype(jnp.float32) + jax.nn.relu(projected)).astype(jnp.bfloat16)

    if section_count == 4 and part_count % 2 == 0:
        pairs = [
            (section * part_count + part, (section ^ 2) * part_count + (part ^ 1))
            for section in range(section_count)
            for part in range(part_count)
        ]
        core_swap = [(0, 1), (1, 0), (2, 3), (3, 2)]

        def spread(value):
            across = lax.ppermute(value, ("section", "dom"), pairs)
            beside_own = lax.ppermute(value, "section", core_swap)
            beside_far = lax.ppermute(across, "section", core_swap)
            return [value, beside_own, across, beside_far]

        def list_index(section):
            return jnp.bitwise_xor(section, group)
    else:
        def spread(value):
            return [value] + [shifted(value, "section", step) for step in range(1, section_count)]

        def list_index(section):
            return (group - section) % section_count

    count_list = jnp.concatenate(spread(layer_counts))
    count_by_section = count_list[list_index(jnp.arange(section_count, dtype=jnp.int32))]
    trips = jnp.clip(count_by_section, 0, slot_total)
    weight_list = spread(weights[0])

    finished = jnp.cumsum(trips)
    total = finished[-1]

    layers = jnp.arange(section_count * slot_total, dtype=jnp.int32)
    layer_section = jnp.sum((finished[None, :] <= layers[:, None]).astype(jnp.int32), axis=1)
    layer_section = jnp.minimum(layer_section, section_count - 1)
    layer_slot = layers - (finished[layer_section] - trips[layer_section])
    layer_slot = jnp.clip(layer_slot, 0, slot_total - 1)
    weight_list_row = list_index(layer_section)

    def weight_for(layer):
        slot = layer_slot[layer]
        picks = [lax.dynamic_index_in_dim(held, slot, 0, keepdims=False) for held in weight_list]
        return lax.select_n(weight_list_row[layer], *picks)

    def recorded(stash, hidden, done):
        return jnp.where((finished == done)[:, None, None], hidden[None], stash)

    stash = jnp.broadcast_to(hidden[None], (section_count,) + hidden.shape)
    normed = normed_of(hidden)

    def layer_step(layer, carry):
        hidden, normed, stash, weight = carry
        hidden = projected_onto(hidden, normed, weight)
        stash = recorded(stash, hidden, layer + 1)
        return hidden, normed_of(hidden), stash, weight_for(layer + 1)

    hidden, normed, stash, weight = lax.fori_loop(
        0, jnp.maximum(total - 1, 0), layer_step, (hidden, normed, stash, weight_for(0))
    )
    hidden = projected_onto(hidden, normed, weight)
    stash = jnp.where(total >= 1, recorded(stash, hidden, total), stash)

    stash_stack = stash
    arrived = [lax.dynamic_index_in_dim(stash_stack, group, 0, keepdims=False)]
    for step in range(1, section_count):
        piece = lax.dynamic_index_in_dim(stash_stack, (group + step) % section_count, 0, keepdims=False)
        arrived.append(shifted(piece, "section", step))
    arrived = jnp.stack(arrived)
    out = arrived[(group - jnp.arange(section_count, dtype=jnp.int32)) % section_count]
    return out[None]


def solution(mesh):
    in_specs = (
        P(None, "dom", None),
        P(None, "dom", None, None),
        P(),
        P("section"),
        P("section", None, None, None),
    )
    out_specs = P("section", None, "dom", None)
    return jax.shard_map(local, mesh=mesh, in_specs=in_specs, out_specs=out_specs, check_vma=False)
```

```python
import jax
import jax.numpy as jnp
from jax import lax
from jax.sharding import PartitionSpec as P


def shifted(value, axis, steps):
    count = lax.axis_size(axis)
    return lax.ppermute(value, axis, [(source, (source + steps) % count) for source in range(count)])


def sent_one_way(value, axis, source, target):
    return lax.ppermute(value, axis, [(source, target)])


def local(features, adjacency, boundary, layer_counts, weights):
    section_count = lax.axis_size("section")
    part_count = lax.axis_size("dom")
    group = lax.axis_index("section")
    part_here = lax.axis_index("dom")
    local_rows = features.shape[1]
    feature_width = features.shape[2]
    local_blocks = adjacency.shape[1]
    block_rows = adjacency.shape[2]
    slot_total = weights.shape[1]

    hidden = lax.dynamic_index_in_dim(features, group, 0, keepdims=False)
    adj_tiles = lax.dynamic_index_in_dim(adjacency, group, 0, keepdims=False)
    bound_ids = lax.dynamic_index_in_dim(boundary, group, 0, keepdims=False)
    send_ids = bound_ids[part_here]
    local_cols = local_blocks * block_rows
    adj_t = adj_tiles.reshape(local_cols, -1).T.reshape(-1, block_rows, local_cols)
    adj_t_local = adj_t[:local_blocks].reshape(local_cols, local_cols)
    adj_t_remote = jnp.concatenate(
        [adj_t[local_blocks:], jnp.zeros((1, block_rows, local_cols), adj_t.dtype)], axis=0
    )
    slot_of_part = (jnp.arange(part_count, dtype=jnp.int32) - part_here - 1) % part_count
    adj_t_by_part = adj_t_remote[slot_of_part].reshape(part_count * block_rows, local_cols)

    def normed_of(hidden):
        local_view = hidden.reshape(local_blocks, block_rows, feature_width)
        outgoing = local_view[send_ids]
        incoming = lax.all_to_all(outgoing, "dom", 0, 0, tiled=True)
        aggregate = jnp.einsum(
            "kb,kd->bd", adj_t_local, hidden, preferred_element_type=jnp.float32
        ) + jnp.einsum(
            "kb,kd->bd", adj_t_by_part, incoming.reshape(-1, feature_width),
            preferred_element_type=jnp.float32,
        )
        mean_square = jnp.mean(aggregate * aggregate, axis=-1, keepdims=True)
        return (aggregate * lax.rsqrt(mean_square + 1e-06)).astype(jnp.bfloat16)

    def projected_onto(hidden, normed, weight):
        projected = jnp.dot(normed, weight, preferred_element_type=jnp.float32)
        return (hidden.astype(jnp.float32) + jax.nn.relu(projected)).astype(jnp.bfloat16)

    if section_count == 4 and part_count % 2 == 0:
        pairs = [
            (section * part_count + part, (section ^ 2) * part_count + (part ^ 1))
            for section in range(section_count)
            for part in range(part_count)
        ]
        core_swap = [(0, 1), (1, 0), (2, 3), (3, 2)]

        def spread(value):
            across = lax.ppermute(value, ("section", "dom"), pairs)
            beside_own = lax.ppermute(value, "section", core_swap)
            beside_far = lax.ppermute(across, "section", core_swap)
            return [value, beside_own, across, beside_far]

        def list_index(section):
            return jnp.bitwise_xor(section, group)
    else:
        def spread(value):
            return [value] + [shifted(value, "section", step) for step in range(1, section_count)]

        def list_index(section):
            return (group - section) % section_count

    extra_rows = 16
    count_here = jnp.clip(layer_counts[0], 0, slot_total).astype(weights.dtype)
    packed = jnp.concatenate(
        [weights[0].reshape(-1, weights.shape[3]), jnp.full((extra_rows, weights.shape[3]), count_here)]
    )
    packed_list = spread(packed)
    weight_rows = slot_total * weights.shape[2]
    count_list = jnp.stack([held[weight_rows, 0] for held in packed_list]).astype(jnp.int32)
    count_by_section = count_list[list_index(jnp.arange(section_count, dtype=jnp.int32))]
    trips = jnp.clip(count_by_section, 0, slot_total)
    weight_list = [held[:weight_rows].reshape(weights.shape[1:]) for held in packed_list]

    finished = jnp.cumsum(trips)
    total = finished[-1]

    layers = jnp.arange(section_count * slot_total, dtype=jnp.int32)
    layer_section = jnp.sum((finished[None, :] <= layers[:, None]).astype(jnp.int32), axis=1)
    layer_section = jnp.minimum(layer_section, section_count - 1)
    layer_slot = layers - (finished[layer_section] - trips[layer_section])
    layer_slot = jnp.clip(layer_slot, 0, slot_total - 1)
    weight_list_row = list_index(layer_section)

    def weight_for(layer):
        slot = layer_slot[layer]
        picks = [lax.dynamic_index_in_dim(held, slot, 0, keepdims=False) for held in weight_list]
        return lax.select_n(weight_list_row[layer], *picks)

    def recorded(stash, hidden, done):
        return jnp.where((finished == done)[:, None, None], hidden[None], stash)

    stash = jnp.broadcast_to(hidden[None], (section_count,) + hidden.shape)
    normed = normed_of(hidden)

    def layer_step(layer, carry):
        hidden, normed, stash, weight = carry
        hidden = projected_onto(hidden, normed, weight)
        stash = recorded(stash, hidden, layer + 1)
        return hidden, normed_of(hidden), stash, weight_for(layer + 1)

    hidden, normed, stash, weight = lax.fori_loop(
        0, jnp.maximum(total - 1, 0), layer_step, (hidden, normed, stash, weight_for(0))
    )
    hidden = projected_onto(hidden, normed, weight)
    stash = jnp.where(total >= 1, recorded(stash, hidden, total), stash)

    stash_stack = stash
    arrived = [lax.dynamic_index_in_dim(stash_stack, group, 0, keepdims=False)]
    for step in range(1, section_count):
        piece = lax.dynamic_index_in_dim(stash_stack, (group + step) % section_count, 0, keepdims=False)
        arrived.append(shifted(piece, "section", step))
    arrived = jnp.stack(arrived)
    out = arrived[(group - jnp.arange(section_count, dtype=jnp.int32)) % section_count]
    return out[None]


def solution(mesh):
    in_specs = (
        P(None, "dom", None),
        P(None, "dom", None, None),
        P(),
        P("section"),
        P("section", None, None, None),
    )
    out_specs = P("section", None, "dom", None)
    return jax.shard_map(local, mesh=mesh, in_specs=in_specs, out_specs=out_specs, check_vma=False)
```

```python
import jax
import jax.numpy as jnp
from jax import lax
from jax.sharding import PartitionSpec as P


def shifted(value, axis, steps):
    count = lax.axis_size(axis)
    return lax.ppermute(value, axis, [(source, (source + steps) % count) for source in range(count)])


def sent_one_way(value, axis, source, target):
    return lax.ppermute(value, axis, [(source, target)])


def local(features, adjacency, boundary, layer_counts, weights):
    section_count = lax.axis_size("section")
    part_count = lax.axis_size("dom")
    group = lax.axis_index("section")
    part_here = lax.axis_index("dom")
    local_rows = features.shape[1]
    feature_width = features.shape[2]
    local_blocks = adjacency.shape[1]
    block_rows = adjacency.shape[2]
    slot_total = weights.shape[1]

    hidden = lax.dynamic_index_in_dim(features, group, 0, keepdims=False)
    adj_tiles = lax.dynamic_index_in_dim(adjacency, group, 0, keepdims=False)
    bound_ids = lax.dynamic_index_in_dim(boundary, group, 0, keepdims=False)
    send_ids = bound_ids[part_here]
    local_cols = local_blocks * block_rows
    adj_t = adj_tiles.reshape(local_cols, -1).T.reshape(-1, block_rows, local_cols)
    adj_t_local = adj_t[:local_blocks].reshape(local_cols, local_cols)
    adj_t_remote = jnp.concatenate(
        [adj_t[local_blocks:], jnp.zeros((1, block_rows, local_cols), adj_t.dtype)], axis=0
    )
    slot_of_part = (jnp.arange(part_count, dtype=jnp.int32) - part_here - 1) % part_count
    adj_t_by_part = adj_t_remote[slot_of_part].reshape(part_count * block_rows, local_cols)

    def normed_of(hidden):
        local_view = hidden.reshape(local_blocks, block_rows, feature_width)
        outgoing = local_view[send_ids]
        incoming = lax.all_to_all(outgoing, "dom", 0, 0, tiled=True)
        aggregate = jnp.einsum(
            "kb,kd->bd", adj_t_local, hidden, preferred_element_type=jnp.float32
        ) + jnp.einsum(
            "kb,kd->bd", adj_t_by_part, incoming.reshape(-1, feature_width),
            preferred_element_type=jnp.float32,
        )
        mean_square = jnp.mean(aggregate * aggregate, axis=-1, keepdims=True)
        return (aggregate * lax.rsqrt(mean_square + 1e-06)).astype(jnp.bfloat16)

    def projected_onto(hidden, normed, weight):
        projected = jnp.dot(normed, weight, preferred_element_type=jnp.float32)
        return (hidden.astype(jnp.float32) + jax.nn.relu(projected)).astype(jnp.bfloat16)

    if section_count == 4 and part_count % 2 == 0:
        pairs = [
            (section * part_count + part, (section ^ 2) * part_count + (part ^ 1))
            for section in range(section_count)
            for part in range(part_count)
        ]
        core_swap = [(0, 1), (1, 0), (2, 3), (3, 2)]

        def spread(value):
            across = lax.ppermute(value, ("section", "dom"), pairs)
            beside_own = lax.ppermute(value, "section", core_swap)
            beside_far = lax.ppermute(across, "section", core_swap)
            return [value, beside_own, across, beside_far]

        def list_index(section):
            return jnp.bitwise_xor(section, group)
    else:
        def spread(value):
            return [value] + [shifted(value, "section", step) for step in range(1, section_count)]

        def list_index(section):
            return (group - section) % section_count

    count_list = jnp.concatenate(spread(layer_counts))
    count_by_section = count_list[list_index(jnp.arange(section_count, dtype=jnp.int32))]
    trips = jnp.clip(count_by_section, 0, slot_total)
    weight_list = spread(weights[0])

    finished = jnp.cumsum(trips)
    total = finished[-1]

    layers = jnp.arange(section_count * slot_total, dtype=jnp.int32)
    layer_section = jnp.sum((finished[None, :] <= layers[:, None]).astype(jnp.int32), axis=1)
    layer_section = jnp.minimum(layer_section, section_count - 1)
    layer_slot = layers - (finished[layer_section] - trips[layer_section])
    layer_slot = jnp.clip(layer_slot, 0, slot_total - 1)
    weight_list_row = list_index(layer_section)

    def weight_for(layer):
        slot = layer_slot[layer]
        picks = [lax.dynamic_index_in_dim(held, slot, 0, keepdims=False) for held in weight_list]
        return lax.select_n(weight_list_row[layer], *picks)

    def recorded(stash, hidden, done):
        return jnp.where((finished == done)[:, None, None], hidden[None], stash)

    stash = jnp.broadcast_to(hidden[None], (section_count,) + hidden.shape)
    normed = normed_of(hidden)

    def layer_step(layer, carry):
        hidden, normed, stash, weight = carry
        hidden = projected_onto(hidden, normed, weight)
        stash = recorded(stash, hidden, layer + 1)
        return hidden, normed_of(hidden), stash, weight_for(layer + 1)

    hidden, normed, stash, weight = lax.fori_loop(
        0, jnp.maximum(total - 1, 0), layer_step, (hidden, normed, stash, weight_for(0))
    )
    hidden = projected_onto(hidden, normed, weight)
    ends_last = (finished == total) & (total >= 1)

    def final_entry(section):
        kept = lax.dynamic_index_in_dim(stash, section, 0, keepdims=False)
        return jnp.where(ends_last[section], hidden, kept)

    arrived = [final_entry(group)]
    for step in range(1, section_count):
        arrived.append(shifted(final_entry((group + step) % section_count), "section", step))
    out = jnp.stack(
        [lax.select_n((group - micro) % section_count, *arrived) for micro in range(section_count)]
    )
    return out[None]


def solution(mesh):
    in_specs = (
        P(None, "dom", None),
        P(None, "dom", None, None),
        P(),
        P("section"),
        P("section", None, None, None),
    )
    out_specs = P("section", None, "dom", None)
    return jax.shard_map(local, mesh=mesh, in_specs=in_specs, out_specs=out_specs, check_vma=False)
```

```python
import jax
import jax.numpy as jnp
from jax import lax
from jax.sharding import PartitionSpec as P


def shifted(value, axis, steps):
    count = lax.axis_size(axis)
    return lax.ppermute(value, axis, [(source, (source + steps) % count) for source in range(count)])


def sent_one_way(value, axis, source, target):
    return lax.ppermute(value, axis, [(source, target)])


def local(features, adjacency, boundary, layer_counts, weights):
    section_count = lax.axis_size("section")
    part_count = lax.axis_size("dom")
    group = lax.axis_index("section")
    part_here = lax.axis_index("dom")
    local_rows = features.shape[1]
    feature_width = features.shape[2]
    local_blocks = adjacency.shape[1]
    block_rows = adjacency.shape[2]
    slot_total = weights.shape[1]

    hidden = lax.dynamic_index_in_dim(features, group, 0, keepdims=False)
    adj_tiles = lax.dynamic_index_in_dim(adjacency, group, 0, keepdims=False)
    bound_ids = lax.dynamic_index_in_dim(boundary, group, 0, keepdims=False)
    send_ids = bound_ids[part_here]
    local_cols = local_blocks * block_rows
    adj_t = adj_tiles.reshape(local_cols, -1).T.reshape(-1, block_rows, local_cols)
    adj_t_local = adj_t[:local_blocks].reshape(local_cols, local_cols)
    adj_t_remote = jnp.concatenate(
        [adj_t[local_blocks:], jnp.zeros((1, block_rows, local_cols), adj_t.dtype)], axis=0
    )
    slot_of_part = (jnp.arange(part_count, dtype=jnp.int32) - part_here - 1) % part_count
    adj_t_by_part = adj_t_remote[slot_of_part].reshape(part_count * block_rows, local_cols)
    adj_local = adj_t_local.T
    adj_by_part = adj_t_by_part.T

    def normed_of(hidden):
        local_view = hidden.reshape(local_blocks, block_rows, feature_width)
        outgoing = local_view[send_ids]
        incoming = lax.all_to_all(outgoing, "dom", 0, 0, tiled=True)
        aggregate = jnp.einsum(
            "bk,kd->bd", adj_local, hidden, preferred_element_type=jnp.float32
        ) + jnp.einsum(
            "bk,kd->bd", adj_by_part, incoming.reshape(-1, feature_width),
            preferred_element_type=jnp.float32,
        )
        mean_square = jnp.mean(aggregate * aggregate, axis=-1, keepdims=True)
        return (aggregate * lax.rsqrt(mean_square + 1e-06)).astype(jnp.bfloat16)

    def projected_onto(hidden, normed, weight):
        projected = jnp.dot(normed, weight, preferred_element_type=jnp.float32)
        return (hidden.astype(jnp.float32) + jax.nn.relu(projected)).astype(jnp.bfloat16)

    if section_count == 4 and part_count % 2 == 0:
        pairs = [
            (section * part_count + part, (section ^ 2) * part_count + (part ^ 1))
            for section in range(section_count)
            for part in range(part_count)
        ]
        core_swap = [(0, 1), (1, 0), (2, 3), (3, 2)]

        def spread(value):
            across = lax.ppermute(value, ("section", "dom"), pairs)
            beside_own = lax.ppermute(value, "section", core_swap)
            beside_far = lax.ppermute(across, "section", core_swap)
            return [value, beside_own, across, beside_far]

        def list_index(section):
            return jnp.bitwise_xor(section, group)
    else:
        def spread(value):
            return [value] + [shifted(value, "section", step) for step in range(1, section_count)]

        def list_index(section):
            return (group - section) % section_count

    count_list = jnp.concatenate(spread(layer_counts))
    count_by_section = count_list[list_index(jnp.arange(section_count, dtype=jnp.int32))]
    trips = jnp.clip(count_by_section, 0, slot_total)
    weight_list = spread(weights[0])

    finished = jnp.cumsum(trips)
    total = finished[-1]

    layers = jnp.arange(section_count * slot_total, dtype=jnp.int32)
    layer_section = jnp.sum((finished[None, :] <= layers[:, None]).astype(jnp.int32), axis=1)
    layer_section = jnp.minimum(layer_section, section_count - 1)
    layer_slot = layers - (finished[layer_section] - trips[layer_section])
    layer_slot = jnp.clip(layer_slot, 0, slot_total - 1)
    weight_list_row = list_index(layer_section)

    def weight_for(layer):
        slot = layer_slot[layer]
        picks = [lax.dynamic_index_in_dim(held, slot, 0, keepdims=False) for held in weight_list]
        return lax.select_n(weight_list_row[layer], *picks)

    def recorded(stash, hidden, done):
        return jnp.where((finished == done)[:, None, None], hidden[None], stash)

    stash = jnp.broadcast_to(hidden[None], (section_count,) + hidden.shape)
    normed = normed_of(hidden)

    def layer_step(layer, carry):
        hidden, normed, stash, weight = carry
        hidden = projected_onto(hidden, normed, weight)
        stash = recorded(stash, hidden, layer + 1)
        return hidden, normed_of(hidden), stash, weight_for(layer + 1)

    hidden, normed, stash, weight = lax.fori_loop(
        0, jnp.maximum(total - 1, 0), layer_step, (hidden, normed, stash, weight_for(0))
    )
    hidden = projected_onto(hidden, normed, weight)
    stash = jnp.where(total >= 1, recorded(stash, hidden, total), stash)

    stash_stack = stash
    arrived = [lax.dynamic_index_in_dim(stash_stack, group, 0, keepdims=False)]
    for step in range(1, section_count):
        piece = lax.dynamic_index_in_dim(stash_stack, (group + step) % section_count, 0, keepdims=False)
        arrived.append(shifted(piece, "section", step))
    arrived = jnp.stack(arrived)
    out = arrived[(group - jnp.arange(section_count, dtype=jnp.int32)) % section_count]
    return out[None]


def solution(mesh):
    in_specs = (
        P(None, "dom", None),
        P(None, "dom", None, None),
        P(),
        P("section"),
        P("section", None, None, None),
    )
    out_specs = P("section", None, "dom", None)
    return jax.shard_map(local, mesh=mesh, in_specs=in_specs, out_specs=out_specs, check_vma=False)
```

```python
import jax
import jax.numpy as jnp
from jax import lax
from jax.experimental import pallas as pl
from jax.experimental.pallas import tpu as pltpu
from jax.sharding import PartitionSpec as P


def layer_kernel(ids_ref, hidden_ref, incoming_ref, adj_local_ref, adj_remote_ref, weight_ref,
                 hidden_out_ref, outgoing_ref):
    hidden = hidden_ref[...]
    aggregate = jnp.dot(adj_local_ref[...], hidden, preferred_element_type=jnp.float32) + jnp.dot(
        adj_remote_ref[...], incoming_ref[...], preferred_element_type=jnp.float32
    )
    mean_square = jnp.mean(aggregate * aggregate, axis=-1, keepdims=True)
    normed = (aggregate * lax.rsqrt(mean_square + 1e-06)).astype(jnp.bfloat16)
    projected = jnp.dot(normed, weight_ref[...], preferred_element_type=jnp.float32)
    updated = (hidden.astype(jnp.float32) + jnp.maximum(projected, 0.0)).astype(jnp.bfloat16)
    hidden_out_ref[...] = updated
    block_rows = outgoing_ref.shape[1]
    first = updated[:block_rows]
    second = updated[block_rows:]
    for part in range(outgoing_ref.shape[0]):
        outgoing_ref[part] = jnp.where(ids_ref[part] == 0, first, second)


def fused_layer(send_ids, hidden, incoming, adj_local, adj_remote, weight):
    parts, block_rows, width = incoming.shape
    vmem = pl.BlockSpec(memory_space=pltpu.VMEM)
    return pl.pallas_call(
        layer_kernel,
        out_shape=(
            jax.ShapeDtypeStruct(hidden.shape, hidden.dtype),
            jax.ShapeDtypeStruct((parts, block_rows, width), hidden.dtype),
        ),
        in_specs=[pl.BlockSpec(memory_space=pltpu.SMEM)] + [vmem] * 5,
        out_specs=(vmem, vmem),
    )(send_ids, hidden, incoming.reshape(parts * block_rows, width), adj_local, adj_remote, weight)


def shifted(value, axis, steps):
    count = lax.axis_size(axis)
    return lax.ppermute(value, axis, [(source, (source + steps) % count) for source in range(count)])


def sent_one_way(value, axis, source, target):
    return lax.ppermute(value, axis, [(source, target)])


def local(features, adjacency, boundary, layer_counts, weights):
    section_count = lax.axis_size("section")
    part_count = lax.axis_size("dom")
    group = lax.axis_index("section")
    part_here = lax.axis_index("dom")
    local_rows = features.shape[1]
    feature_width = features.shape[2]
    local_blocks = adjacency.shape[1]
    block_rows = adjacency.shape[2]
    slot_total = weights.shape[1]

    hidden = lax.dynamic_index_in_dim(features, group, 0, keepdims=False)
    adj_tiles = lax.dynamic_index_in_dim(adjacency, group, 0, keepdims=False)
    bound_ids = lax.dynamic_index_in_dim(boundary, group, 0, keepdims=False)
    send_ids = bound_ids[part_here]
    local_cols = local_blocks * block_rows
    adj_t = adj_tiles.reshape(local_cols, -1).T.reshape(-1, block_rows, local_cols)
    adj_t_local = adj_t[:local_blocks].reshape(local_cols, local_cols)
    adj_t_remote = jnp.concatenate(
        [adj_t[local_blocks:], jnp.zeros((1, block_rows, local_cols), adj_t.dtype)], axis=0
    )
    slot_of_part = (jnp.arange(part_count, dtype=jnp.int32) - part_here - 1) % part_count
    adj_t_by_part = adj_t_remote[slot_of_part].reshape(part_count * block_rows, local_cols)
    adj_local = adj_t_local.T
    adj_by_part = adj_t_by_part.T

    def normed_of(hidden):
        local_view = hidden.reshape(local_blocks, block_rows, feature_width)
        outgoing = local_view[send_ids]
        incoming = lax.all_to_all(outgoing, "dom", 0, 0, tiled=True)
        aggregate = jnp.einsum(
            "kb,kd->bd", adj_t_local, hidden, preferred_element_type=jnp.float32
        ) + jnp.einsum(
            "kb,kd->bd", adj_t_by_part, incoming.reshape(-1, feature_width),
            preferred_element_type=jnp.float32,
        )
        mean_square = jnp.mean(aggregate * aggregate, axis=-1, keepdims=True)
        return (aggregate * lax.rsqrt(mean_square + 1e-06)).astype(jnp.bfloat16)

    def projected_onto(hidden, normed, weight):
        projected = jnp.dot(normed, weight, preferred_element_type=jnp.float32)
        return (hidden.astype(jnp.float32) + jax.nn.relu(projected)).astype(jnp.bfloat16)

    if section_count == 4 and part_count % 2 == 0:
        pairs = [
            (section * part_count + part, (section ^ 2) * part_count + (part ^ 1))
            for section in range(section_count)
            for part in range(part_count)
        ]
        core_swap = [(0, 1), (1, 0), (2, 3), (3, 2)]

        def spread(value):
            across = lax.ppermute(value, ("section", "dom"), pairs)
            beside_own = lax.ppermute(value, "section", core_swap)
            beside_far = lax.ppermute(across, "section", core_swap)
            return [value, beside_own, across, beside_far]

        def list_index(section):
            return jnp.bitwise_xor(section, group)
    else:
        def spread(value):
            return [value] + [shifted(value, "section", step) for step in range(1, section_count)]

        def list_index(section):
            return (group - section) % section_count

    count_list = jnp.concatenate(spread(layer_counts))
    count_by_section = count_list[list_index(jnp.arange(section_count, dtype=jnp.int32))]
    trips = jnp.clip(count_by_section, 0, slot_total)
    weight_list = spread(weights[0])

    finished = jnp.cumsum(trips)
    total = finished[-1]

    layers = jnp.arange(section_count * slot_total, dtype=jnp.int32)
    layer_section = jnp.sum((finished[None, :] <= layers[:, None]).astype(jnp.int32), axis=1)
    layer_section = jnp.minimum(layer_section, section_count - 1)
    layer_slot = layers - (finished[layer_section] - trips[layer_section])
    layer_slot = jnp.clip(layer_slot, 0, slot_total - 1)
    weight_list_row = list_index(layer_section)

    def weight_for(layer):
        slot = layer_slot[layer]
        picks = [lax.dynamic_index_in_dim(held, slot, 0, keepdims=False) for held in weight_list]
        return lax.select_n(weight_list_row[layer], *picks)

    def recorded(stash, hidden, done):
        return jnp.where((finished == done)[:, None, None], hidden[None], stash)

    stash = jnp.broadcast_to(hidden[None], (section_count,) + hidden.shape)

    def exchanged(outgoing):
        return lax.all_to_all(outgoing, "dom", 0, 0, tiled=True)

    first_outgoing = hidden.reshape(local_blocks, block_rows, feature_width)[send_ids]
    incoming = exchanged(first_outgoing)

    def layer_step(layer, carry):
        hidden, incoming, stash, weight = carry
        hidden, outgoing = fused_layer(send_ids, hidden, incoming, adj_local, adj_by_part, weight)
        stash = recorded(stash, hidden, layer + 1)
        return hidden, exchanged(outgoing), stash, weight_for(layer + 1)

    hidden, incoming, stash, weight = lax.fori_loop(
        0, jnp.maximum(total - 1, 0), layer_step, (hidden, incoming, stash, weight_for(0))
    )
    hidden = fused_layer(send_ids, hidden, incoming, adj_local, adj_by_part, weight)[0]
    stash = jnp.where(total >= 1, recorded(stash, hidden, total), stash)

    stash_stack = stash
    arrived = [lax.dynamic_index_in_dim(stash_stack, group, 0, keepdims=False)]
    for step in range(1, section_count):
        piece = lax.dynamic_index_in_dim(stash_stack, (group + step) % section_count, 0, keepdims=False)
        arrived.append(shifted(piece, "section", step))
    arrived = jnp.stack(arrived)
    out = arrived[(group - jnp.arange(section_count, dtype=jnp.int32)) % section_count]
    return out[None]


def solution(mesh):
    in_specs = (
        P(None, "dom", None),
        P(None, "dom", None, None),
        P(),
        P("section"),
        P("section", None, None, None),
    )
    out_specs = P("section", None, "dom", None)
    return jax.shard_map(local, mesh=mesh, in_specs=in_specs, out_specs=out_specs, check_vma=False)
```

```python
import jax
import jax.numpy as jnp
from jax import lax
from jax.experimental import pallas as pl
from jax.experimental.pallas import tpu as pltpu
from jax.sharding import PartitionSpec as P


def layer_kernel(ids_ref, hidden_ref, incoming_ref, adj_local_ref, adj_remote_ref, weight_ref,
                 hidden_out_ref, outgoing_ref):
    hidden = hidden_ref[...]
    aggregate = jnp.dot(adj_local_ref[...], hidden, preferred_element_type=jnp.float32) + jnp.dot(
        adj_remote_ref[...], incoming_ref[...], preferred_element_type=jnp.float32
    )
    mean_square = jnp.mean(aggregate * aggregate, axis=-1, keepdims=True)
    normed = (aggregate * lax.rsqrt(mean_square + 1e-06)).astype(jnp.bfloat16)
    projected = jnp.dot(normed, weight_ref[...], preferred_element_type=jnp.float32)
    updated = (hidden.astype(jnp.float32) + jnp.maximum(projected, 0.0)).astype(jnp.bfloat16)
    hidden_out_ref[...] = updated
    block_rows = outgoing_ref.shape[1]
    first = updated[:block_rows]
    second = updated[block_rows:]
    for part in range(outgoing_ref.shape[0]):
        outgoing_ref[part] = jnp.where(ids_ref[part] == 0, first, second)


def fused_layer(send_ids, hidden, incoming, adj_local, adj_remote, weight):
    parts, block_rows, width = incoming.shape
    vmem = pl.BlockSpec(memory_space=pltpu.VMEM)
    return pl.pallas_call(
        layer_kernel,
        out_shape=(
            jax.ShapeDtypeStruct(hidden.shape, hidden.dtype),
            jax.ShapeDtypeStruct((parts, block_rows, width), hidden.dtype),
        ),
        in_specs=[pl.BlockSpec(memory_space=pltpu.SMEM)] + [vmem] * 5,
        out_specs=(vmem, vmem),
        input_output_aliases={1: 0},
    )(send_ids, hidden, incoming.reshape(parts * block_rows, width), adj_local, adj_remote, weight)


def shifted(value, axis, steps):
    count = lax.axis_size(axis)
    return lax.ppermute(value, axis, [(source, (source + steps) % count) for source in range(count)])


def sent_one_way(value, axis, source, target):
    return lax.ppermute(value, axis, [(source, target)])


def local(features, adjacency, boundary, layer_counts, weights):
    section_count = lax.axis_size("section")
    part_count = lax.axis_size("dom")
    group = lax.axis_index("section")
    part_here = lax.axis_index("dom")
    local_rows = features.shape[1]
    feature_width = features.shape[2]
    local_blocks = adjacency.shape[1]
    block_rows = adjacency.shape[2]
    slot_total = weights.shape[1]

    hidden = lax.dynamic_index_in_dim(features, group, 0, keepdims=False)
    adj_tiles = lax.dynamic_index_in_dim(adjacency, group, 0, keepdims=False)
    bound_ids = lax.dynamic_index_in_dim(boundary, group, 0, keepdims=False)
    send_ids = bound_ids[part_here]
    local_cols = local_blocks * block_rows
    adj_t = adj_tiles.reshape(local_cols, -1).T.reshape(-1, block_rows, local_cols)
    adj_t_local = adj_t[:local_blocks].reshape(local_cols, local_cols)
    adj_t_remote = jnp.concatenate(
        [adj_t[local_blocks:], jnp.zeros((1, block_rows, local_cols), adj_t.dtype)], axis=0
    )
    slot_of_part = (jnp.arange(part_count, dtype=jnp.int32) - part_here - 1) % part_count
    adj_t_by_part = adj_t_remote[slot_of_part].reshape(part_count * block_rows, local_cols)
    adj_local = adj_t_local.T
    adj_by_part = adj_t_by_part.T

    def normed_of(hidden):
        local_view = hidden.reshape(local_blocks, block_rows, feature_width)
        outgoing = local_view[send_ids]
        incoming = lax.all_to_all(outgoing, "dom", 0, 0, tiled=True)
        aggregate = jnp.einsum(
            "kb,kd->bd", adj_t_local, hidden, preferred_element_type=jnp.float32
        ) + jnp.einsum(
            "kb,kd->bd", adj_t_by_part, incoming.reshape(-1, feature_width),
            preferred_element_type=jnp.float32,
        )
        mean_square = jnp.mean(aggregate * aggregate, axis=-1, keepdims=True)
        return (aggregate * lax.rsqrt(mean_square + 1e-06)).astype(jnp.bfloat16)

    def projected_onto(hidden, normed, weight):
        projected = jnp.dot(normed, weight, preferred_element_type=jnp.float32)
        return (hidden.astype(jnp.float32) + jax.nn.relu(projected)).astype(jnp.bfloat16)

    if section_count == 4 and part_count % 2 == 0:
        pairs = [
            (section * part_count + part, (section ^ 2) * part_count + (part ^ 1))
            for section in range(section_count)
            for part in range(part_count)
        ]
        core_swap = [(0, 1), (1, 0), (2, 3), (3, 2)]

        def spread(value):
            across = lax.ppermute(value, ("section", "dom"), pairs)
            beside_own = lax.ppermute(value, "section", core_swap)
            beside_far = lax.ppermute(across, "section", core_swap)
            return [value, beside_own, across, beside_far]

        def list_index(section):
            return jnp.bitwise_xor(section, group)
    else:
        def spread(value):
            return [value] + [shifted(value, "section", step) for step in range(1, section_count)]

        def list_index(section):
            return (group - section) % section_count

    count_list = jnp.concatenate(spread(layer_counts))
    count_by_section = count_list[list_index(jnp.arange(section_count, dtype=jnp.int32))]
    trips = jnp.clip(count_by_section, 0, slot_total)
    weight_list = spread(weights[0])

    finished = jnp.cumsum(trips)
    total = finished[-1]

    layers = jnp.arange(section_count * slot_total, dtype=jnp.int32)
    layer_section = jnp.sum((finished[None, :] <= layers[:, None]).astype(jnp.int32), axis=1)
    layer_section = jnp.minimum(layer_section, section_count - 1)
    layer_slot = layers - (finished[layer_section] - trips[layer_section])
    layer_slot = jnp.clip(layer_slot, 0, slot_total - 1)
    weight_list_row = list_index(layer_section)

    def weight_for(layer):
        slot = layer_slot[layer]
        picks = [lax.dynamic_index_in_dim(held, slot, 0, keepdims=False) for held in weight_list]
        return lax.select_n(weight_list_row[layer], *picks)

    def recorded(stash, hidden, done):
        return jnp.where((finished == done)[:, None, None], hidden[None], stash)

    stash = jnp.broadcast_to(hidden[None], (section_count,) + hidden.shape)

    def exchanged(outgoing):
        return lax.all_to_all(outgoing, "dom", 0, 0, tiled=True)

    first_outgoing = hidden.reshape(local_blocks, block_rows, feature_width)[send_ids]
    incoming = exchanged(first_outgoing)

    def layer_step(layer, carry):
        hidden, incoming, stash, weight = carry
        hidden, outgoing = fused_layer(send_ids, hidden, incoming, adj_local, adj_by_part, weight)
        stash = recorded(stash, hidden, layer + 1)
        return hidden, exchanged(outgoing), stash, weight_for(layer + 1)

    hidden, incoming, stash, weight = lax.fori_loop(
        0, jnp.maximum(total - 1, 0), layer_step, (hidden, incoming, stash, weight_for(0))
    )
    hidden = fused_layer(send_ids, hidden, incoming, adj_local, adj_by_part, weight)[0]
    stash = jnp.where(total >= 1, recorded(stash, hidden, total), stash)

    stash_stack = stash
    arrived = [lax.dynamic_index_in_dim(stash_stack, group, 0, keepdims=False)]
    for step in range(1, section_count):
        piece = lax.dynamic_index_in_dim(stash_stack, (group + step) % section_count, 0, keepdims=False)
        arrived.append(shifted(piece, "section", step))
    arrived = jnp.stack(arrived)
    out = arrived[(group - jnp.arange(section_count, dtype=jnp.int32)) % section_count]
    return out[None]


def solution(mesh):
    in_specs = (
        P(None, "dom", None),
        P(None, "dom", None, None),
        P(),
        P("section"),
        P("section", None, None, None),
    )
    out_specs = P("section", None, "dom", None)
    return jax.shard_map(local, mesh=mesh, in_specs=in_specs, out_specs=out_specs, check_vma=False)
```

```python
import jax
import jax.numpy as jnp
from jax import lax
from jax.experimental import pallas as pl
from jax.experimental.pallas import tpu as pltpu
from jax.sharding import PartitionSpec as P


def layer_kernel(ids_ref, hidden_ref, incoming_ref, adj_local_ref, adj_remote_ref, weight_ref,
                 hidden_out_ref, outgoing_ref=None):
    hidden = hidden_ref[...]
    aggregate = jnp.dot(adj_local_ref[...], hidden, preferred_element_type=jnp.float32) + jnp.dot(
        adj_remote_ref[...], incoming_ref[...], preferred_element_type=jnp.float32
    )
    mean_square = jnp.mean(aggregate * aggregate, axis=-1, keepdims=True)
    normed = (aggregate * lax.rsqrt(mean_square + 1e-06)).astype(jnp.bfloat16)
    projected = jnp.dot(normed, weight_ref[...], preferred_element_type=jnp.float32)
    updated = (hidden.astype(jnp.float32) + jnp.maximum(projected, 0.0)).astype(jnp.bfloat16)
    hidden_out_ref[...] = updated
    if outgoing_ref is None:
        return
    block_rows = outgoing_ref.shape[1]
    first = updated[:block_rows]
    second = updated[block_rows:]
    for part in range(outgoing_ref.shape[0]):
        outgoing_ref[part] = jnp.where(ids_ref[part] == 0, first, second)


def fused_layer(send_ids, hidden, incoming, adj_local, adj_remote, weight, with_outgoing=True):
    parts, block_rows, width = incoming.shape
    vmem = pl.BlockSpec(memory_space=pltpu.VMEM)
    hidden_shape = jax.ShapeDtypeStruct(hidden.shape, hidden.dtype)
    if with_outgoing:
        out_shape = (hidden_shape, jax.ShapeDtypeStruct((parts, block_rows, width), hidden.dtype))
        out_specs = (vmem, vmem)
    else:
        out_shape = (hidden_shape,)
        out_specs = (vmem,)
    return pl.pallas_call(
        layer_kernel,
        out_shape=out_shape,
        in_specs=[pl.BlockSpec(memory_space=pltpu.SMEM)] + [vmem] * 5,
        out_specs=out_specs,
        input_output_aliases={1: 0},
    )(send_ids, hidden, incoming.reshape(parts * block_rows, width), adj_local, adj_remote, weight)


def shifted(value, axis, steps):
    count = lax.axis_size(axis)
    return lax.ppermute(value, axis, [(source, (source + steps) % count) for source in range(count)])


def sent_one_way(value, axis, source, target):
    return lax.ppermute(value, axis, [(source, target)])


def local(features, adjacency, boundary, layer_counts, weights):
    section_count = lax.axis_size("section")
    part_count = lax.axis_size("dom")
    group = lax.axis_index("section")
    part_here = lax.axis_index("dom")
    local_rows = features.shape[1]
    feature_width = features.shape[2]
    local_blocks = adjacency.shape[1]
    block_rows = adjacency.shape[2]
    slot_total = weights.shape[1]

    hidden = lax.dynamic_index_in_dim(features, group, 0, keepdims=False)
    adj_tiles = lax.dynamic_index_in_dim(adjacency, group, 0, keepdims=False)
    bound_ids = lax.dynamic_index_in_dim(boundary, group, 0, keepdims=False)
    send_ids = bound_ids[part_here]
    local_cols = local_blocks * block_rows
    adj_t = adj_tiles.reshape(local_cols, -1).T.reshape(-1, block_rows, local_cols)
    adj_t_local = adj_t[:local_blocks].reshape(local_cols, local_cols)
    adj_t_remote = jnp.concatenate(
        [adj_t[local_blocks:], jnp.zeros((1, block_rows, local_cols), adj_t.dtype)], axis=0
    )
    slot_of_part = (jnp.arange(part_count, dtype=jnp.int32) - part_here - 1) % part_count
    adj_t_by_part = adj_t_remote[slot_of_part].reshape(part_count * block_rows, local_cols)
    adj_local = adj_t_local.T
    adj_by_part = adj_t_by_part.T

    def normed_of(hidden):
        local_view = hidden.reshape(local_blocks, block_rows, feature_width)
        outgoing = local_view[send_ids]
        incoming = lax.all_to_all(outgoing, "dom", 0, 0, tiled=True)
        aggregate = jnp.einsum(
            "kb,kd->bd", adj_t_local, hidden, preferred_element_type=jnp.float32
        ) + jnp.einsum(
            "kb,kd->bd", adj_t_by_part, incoming.reshape(-1, feature_width),
            preferred_element_type=jnp.float32,
        )
        mean_square = jnp.mean(aggregate * aggregate, axis=-1, keepdims=True)
        return (aggregate * lax.rsqrt(mean_square + 1e-06)).astype(jnp.bfloat16)

    def projected_onto(hidden, normed, weight):
        projected = jnp.dot(normed, weight, preferred_element_type=jnp.float32)
        return (hidden.astype(jnp.float32) + jax.nn.relu(projected)).astype(jnp.bfloat16)

    if section_count == 4 and part_count % 2 == 0:
        pairs = [
            (section * part_count + part, (section ^ 2) * part_count + (part ^ 1))
            for section in range(section_count)
            for part in range(part_count)
        ]
        core_swap = [(0, 1), (1, 0), (2, 3), (3, 2)]

        def spread(value):
            across = lax.ppermute(value, ("section", "dom"), pairs)
            beside_own = lax.ppermute(value, "section", core_swap)
            beside_far = lax.ppermute(across, "section", core_swap)
            return [value, beside_own, across, beside_far]

        def list_index(section):
            return jnp.bitwise_xor(section, group)
    else:
        def spread(value):
            return [value] + [shifted(value, "section", step) for step in range(1, section_count)]

        def list_index(section):
            return (group - section) % section_count

    count_list = jnp.concatenate(spread(layer_counts))
    count_by_section = count_list[list_index(jnp.arange(section_count, dtype=jnp.int32))]
    trips = jnp.clip(count_by_section, 0, slot_total)
    weight_list = spread(weights[0])

    finished = jnp.cumsum(trips)
    total = finished[-1]

    layers = jnp.arange(section_count * slot_total, dtype=jnp.int32)
    layer_section = jnp.sum((finished[None, :] <= layers[:, None]).astype(jnp.int32), axis=1)
    layer_section = jnp.minimum(layer_section, section_count - 1)
    layer_slot = layers - (finished[layer_section] - trips[layer_section])
    layer_slot = jnp.clip(layer_slot, 0, slot_total - 1)
    weight_list_row = list_index(layer_section)

    def weight_for(layer):
        slot = layer_slot[layer]
        picks = [lax.dynamic_index_in_dim(held, slot, 0, keepdims=False) for held in weight_list]
        return lax.select_n(weight_list_row[layer], *picks)

    def recorded(stash, hidden, done):
        return jnp.where((finished == done)[:, None, None], hidden[None], stash)

    stash = jnp.broadcast_to(hidden[None], (section_count,) + hidden.shape)

    def exchanged(outgoing):
        return lax.all_to_all(outgoing, "dom", 0, 0, tiled=True)

    first_outgoing = hidden.reshape(local_blocks, block_rows, feature_width)[send_ids]
    incoming = exchanged(first_outgoing)

    def layer_step(layer, carry):
        hidden, incoming, stash, weight = carry
        hidden, outgoing = fused_layer(send_ids, hidden, incoming, adj_local, adj_by_part, weight)
        stash = recorded(stash, hidden, layer + 1)
        return hidden, exchanged(outgoing), stash, weight_for(layer + 1)

    hidden, incoming, stash, weight = lax.fori_loop(
        0, jnp.maximum(total - 1, 0), layer_step, (hidden, incoming, stash, weight_for(0))
    )
    hidden = fused_layer(send_ids, hidden, incoming, adj_local, adj_by_part, weight, with_outgoing=False)[0]
    stash = jnp.where(total >= 1, recorded(stash, hidden, total), stash)

    stash_stack = stash
    arrived = [lax.dynamic_index_in_dim(stash_stack, group, 0, keepdims=False)]
    for step in range(1, section_count):
        piece = lax.dynamic_index_in_dim(stash_stack, (group + step) % section_count, 0, keepdims=False)
        arrived.append(shifted(piece, "section", step))
    arrived = jnp.stack(arrived)
    out = arrived[(group - jnp.arange(section_count, dtype=jnp.int32)) % section_count]
    return out[None]


def solution(mesh):
    in_specs = (
        P(None, "dom", None),
        P(None, "dom", None, None),
        P(),
        P("section"),
        P("section", None, None, None),
    )
    out_specs = P("section", None, "dom", None)
    return jax.shard_map(local, mesh=mesh, in_specs=in_specs, out_specs=out_specs, check_vma=False)
```

```python
import jax
import jax.numpy as jnp
from jax import lax
from jax.experimental import pallas as pl
from jax.experimental.pallas import tpu as pltpu
from jax.sharding import PartitionSpec as P


INCOMING_CHUNKS = 4


def layer_kernel(ids_ref, hidden_ref, incoming_hbm, adj_local_ref, adj_remote_ref, weight_ref,
                 hidden_out_ref, *rest):
    outgoing_ref = rest[0] if len(rest) == 3 else None
    landed, arrived = rest[-2], rest[-1]
    rows = landed.shape[0] // INCOMING_CHUNKS
    copies = [
        pltpu.make_async_copy(
            incoming_hbm.at[pl.ds(chunk * rows, rows)], landed.at[pl.ds(chunk * rows, rows)], arrived.at[chunk]
        )
        for chunk in range(INCOMING_CHUNKS)
    ]
    for copy in copies:
        copy.start()
    hidden = hidden_ref[...]
    aggregate = jnp.dot(adj_local_ref[...], hidden, preferred_element_type=jnp.float32)
    for chunk, copy in enumerate(copies):
        copy.wait()
        aggregate = aggregate + jnp.dot(
            adj_remote_ref[:, pl.ds(chunk * rows, rows)], landed[pl.ds(chunk * rows, rows), :],
            preferred_element_type=jnp.float32,
        )
    mean_square = jnp.mean(aggregate * aggregate, axis=-1, keepdims=True)
    normed = (aggregate * lax.rsqrt(mean_square + 1e-06)).astype(jnp.bfloat16)
    projected = jnp.dot(normed, weight_ref[...], preferred_element_type=jnp.float32)
    updated = (hidden.astype(jnp.float32) + jnp.maximum(projected, 0.0)).astype(jnp.bfloat16)
    hidden_out_ref[...] = updated
    if outgoing_ref is None:
        return
    block_rows = outgoing_ref.shape[1]
    first = updated[:block_rows]
    second = updated[block_rows:]
    for part in range(outgoing_ref.shape[0]):
        outgoing_ref[part] = jnp.where(ids_ref[part] == 0, first, second)


def fused_layer(send_ids, hidden, incoming, adj_local, adj_remote, weight, with_outgoing=True):
    parts, block_rows, width = incoming.shape
    vmem = pl.BlockSpec(memory_space=pltpu.VMEM)
    hidden_shape = jax.ShapeDtypeStruct(hidden.shape, hidden.dtype)
    if with_outgoing:
        out_shape = (hidden_shape, jax.ShapeDtypeStruct((parts, block_rows, width), hidden.dtype))
        out_specs = (vmem, vmem)
    else:
        out_shape = (hidden_shape,)
        out_specs = (vmem,)
    return pl.pallas_call(
        layer_kernel,
        out_shape=out_shape,
        in_specs=[pl.BlockSpec(memory_space=pltpu.SMEM), vmem, pl.BlockSpec(memory_space=pl.ANY)]
        + [vmem] * 3,
        out_specs=out_specs,
        scratch_shapes=[
            pltpu.VMEM((parts * block_rows, width), incoming.dtype),
            pltpu.SemaphoreType.DMA((INCOMING_CHUNKS,)),
        ],
        input_output_aliases={1: 0},
    )(send_ids, hidden, incoming.reshape(parts * block_rows, width), adj_local, adj_remote, weight)


def shifted(value, axis, steps):
    count = lax.axis_size(axis)
    return lax.ppermute(value, axis, [(source, (source + steps) % count) for source in range(count)])


def sent_one_way(value, axis, source, target):
    return lax.ppermute(value, axis, [(source, target)])


def local(features, adjacency, boundary, layer_counts, weights):
    section_count = lax.axis_size("section")
    part_count = lax.axis_size("dom")
    group = lax.axis_index("section")
    part_here = lax.axis_index("dom")
    local_rows = features.shape[1]
    feature_width = features.shape[2]
    local_blocks = adjacency.shape[1]
    block_rows = adjacency.shape[2]
    slot_total = weights.shape[1]

    hidden = lax.dynamic_index_in_dim(features, group, 0, keepdims=False)
    adj_tiles = lax.dynamic_index_in_dim(adjacency, group, 0, keepdims=False)
    bound_ids = lax.dynamic_index_in_dim(boundary, group, 0, keepdims=False)
    send_ids = bound_ids[part_here]
    local_cols = local_blocks * block_rows
    adj_t = adj_tiles.reshape(local_cols, -1).T.reshape(-1, block_rows, local_cols)
    adj_t_local = adj_t[:local_blocks].reshape(local_cols, local_cols)
    adj_t_remote = jnp.concatenate(
        [adj_t[local_blocks:], jnp.zeros((1, block_rows, local_cols), adj_t.dtype)], axis=0
    )
    slot_of_part = (jnp.arange(part_count, dtype=jnp.int32) - part_here - 1) % part_count
    adj_t_by_part = adj_t_remote[slot_of_part].reshape(part_count * block_rows, local_cols)
    adj_local = adj_t_local.T
    adj_by_part = adj_t_by_part.T

    def normed_of(hidden):
        local_view = hidden.reshape(local_blocks, block_rows, feature_width)
        outgoing = local_view[send_ids]
        incoming = lax.all_to_all(outgoing, "dom", 0, 0, tiled=True)
        aggregate = jnp.einsum(
            "kb,kd->bd", adj_t_local, hidden, preferred_element_type=jnp.float32
        ) + jnp.einsum(
            "kb,kd->bd", adj_t_by_part, incoming.reshape(-1, feature_width),
            preferred_element_type=jnp.float32,
        )
        mean_square = jnp.mean(aggregate * aggregate, axis=-1, keepdims=True)
        return (aggregate * lax.rsqrt(mean_square + 1e-06)).astype(jnp.bfloat16)

    def projected_onto(hidden, normed, weight):
        projected = jnp.dot(normed, weight, preferred_element_type=jnp.float32)
        return (hidden.astype(jnp.float32) + jax.nn.relu(projected)).astype(jnp.bfloat16)

    if section_count == 4 and part_count % 2 == 0:
        pairs = [
            (section * part_count + part, (section ^ 2) * part_count + (part ^ 1))
            for section in range(section_count)
            for part in range(part_count)
        ]
        core_swap = [(0, 1), (1, 0), (2, 3), (3, 2)]

        def spread(value):
            across = lax.ppermute(value, ("section", "dom"), pairs)
            beside_own = lax.ppermute(value, "section", core_swap)
            beside_far = lax.ppermute(across, "section", core_swap)
            return [value, beside_own, across, beside_far]

        def list_index(section):
            return jnp.bitwise_xor(section, group)
    else:
        def spread(value):
            return [value] + [shifted(value, "section", step) for step in range(1, section_count)]

        def list_index(section):
            return (group - section) % section_count

    count_list = jnp.concatenate(spread(layer_counts))
    count_by_section = count_list[list_index(jnp.arange(section_count, dtype=jnp.int32))]
    trips = jnp.clip(count_by_section, 0, slot_total)
    weight_list = spread(weights[0])

    finished = jnp.cumsum(trips)
    total = finished[-1]

    layers = jnp.arange(section_count * slot_total, dtype=jnp.int32)
    layer_section = jnp.sum((finished[None, :] <= layers[:, None]).astype(jnp.int32), axis=1)
    layer_section = jnp.minimum(layer_section, section_count - 1)
    layer_slot = layers - (finished[layer_section] - trips[layer_section])
    layer_slot = jnp.clip(layer_slot, 0, slot_total - 1)
    weight_list_row = list_index(layer_section)

    def weight_for(layer):
        slot = layer_slot[layer]
        picks = [lax.dynamic_index_in_dim(held, slot, 0, keepdims=False) for held in weight_list]
        return lax.select_n(weight_list_row[layer], *picks)

    def recorded(stash, hidden, done):
        return jnp.where((finished == done)[:, None, None], hidden[None], stash)

    stash = jnp.broadcast_to(hidden[None], (section_count,) + hidden.shape)

    def exchanged(outgoing):
        return lax.all_to_all(outgoing, "dom", 0, 0, tiled=True)

    first_outgoing = hidden.reshape(local_blocks, block_rows, feature_width)[send_ids]
    incoming = exchanged(first_outgoing)

    def layer_step(layer, carry):
        hidden, incoming, stash, weight = carry
        hidden, outgoing = fused_layer(send_ids, hidden, incoming, adj_local, adj_by_part, weight)
        stash = recorded(stash, hidden, layer + 1)
        return hidden, exchanged(outgoing), stash, weight_for(layer + 1)

    hidden, incoming, stash, weight = lax.fori_loop(
        0, jnp.maximum(total - 1, 0), layer_step, (hidden, incoming, stash, weight_for(0))
    )
    hidden = fused_layer(send_ids, hidden, incoming, adj_local, adj_by_part, weight, with_outgoing=False)[0]
    stash = jnp.where(total >= 1, recorded(stash, hidden, total), stash)

    stash_stack = stash
    arrived = [lax.dynamic_index_in_dim(stash_stack, group, 0, keepdims=False)]
    for step in range(1, section_count):
        piece = lax.dynamic_index_in_dim(stash_stack, (group + step) % section_count, 0, keepdims=False)
        arrived.append(shifted(piece, "section", step))
    arrived = jnp.stack(arrived)
    out = arrived[(group - jnp.arange(section_count, dtype=jnp.int32)) % section_count]
    return out[None]


def solution(mesh):
    in_specs = (
        P(None, "dom", None),
        P(None, "dom", None, None),
        P(),
        P("section"),
        P("section", None, None, None),
    )
    out_specs = P("section", None, "dom", None)
    return jax.shard_map(local, mesh=mesh, in_specs=in_specs, out_specs=out_specs, check_vma=False)
```

```python
import jax
import jax.numpy as jnp
from jax import lax
from jax.experimental import pallas as pl
from jax.experimental.pallas import tpu as pltpu
from jax.sharding import PartitionSpec as P


def layer_kernel(ids_ref, hidden_ref, incoming_ref, adj_local_ref, adj_remote_ref, weight_ref,
                 hidden_out_ref, outgoing_ref=None):
    hidden = hidden_ref[...]
    aggregate = jnp.dot(adj_local_ref[...], hidden, preferred_element_type=jnp.float32) + jnp.dot(
        adj_remote_ref[...], incoming_ref[...], preferred_element_type=jnp.float32
    )
    mean_square = jnp.mean(aggregate * aggregate, axis=-1, keepdims=True)
    normed = (aggregate * lax.rsqrt(mean_square + 1e-06)).astype(jnp.bfloat16)
    projected = jnp.dot(normed, weight_ref[...], preferred_element_type=jnp.float32)
    updated = (hidden.astype(jnp.float32) + jnp.maximum(projected, 0.0)).astype(jnp.bfloat16)
    hidden_out_ref[...] = updated
    if outgoing_ref is None:
        return
    block_rows = outgoing_ref.shape[1]
    first = updated[:block_rows]
    second = updated[block_rows:]
    for part in range(outgoing_ref.shape[0]):
        outgoing_ref[part] = jnp.where(ids_ref[part] == 0, first, second)


def fused_layer(send_ids, hidden, incoming, adj_local, adj_remote, weight, with_outgoing=True):
    parts, block_rows, width = incoming.shape
    vmem = pl.BlockSpec(memory_space=pltpu.VMEM)
    hidden_shape = jax.ShapeDtypeStruct(hidden.shape, hidden.dtype)
    if with_outgoing:
        out_shape = (hidden_shape, jax.ShapeDtypeStruct((parts, block_rows, width), hidden.dtype))
        out_specs = (vmem, vmem)
    else:
        out_shape = (hidden_shape,)
        out_specs = (vmem,)
    return pl.pallas_call(
        layer_kernel,
        out_shape=out_shape,
        in_specs=[pl.BlockSpec(memory_space=pltpu.SMEM)] + [vmem] * 5,
        out_specs=out_specs,
        input_output_aliases={1: 0},
    )(send_ids, hidden, incoming.reshape(parts * block_rows, width), adj_local, adj_remote, weight)


def shifted(value, axis, steps):
    count = lax.axis_size(axis)
    return lax.ppermute(value, axis, [(source, (source + steps) % count) for source in range(count)])


def sent_one_way(value, axis, source, target):
    return lax.ppermute(value, axis, [(source, target)])


def local(features, adjacency, boundary, layer_counts, weights):
    section_count = lax.axis_size("section")
    part_count = lax.axis_size("dom")
    group = lax.axis_index("section")
    part_here = lax.axis_index("dom")
    local_rows = features.shape[1]
    feature_width = features.shape[2]
    local_blocks = adjacency.shape[1]
    block_rows = adjacency.shape[2]
    slot_total = weights.shape[1]

    hidden = lax.dynamic_index_in_dim(features, group, 0, keepdims=False)
    adj_tiles = lax.dynamic_index_in_dim(adjacency, group, 0, keepdims=False)
    bound_ids = lax.dynamic_index_in_dim(boundary, group, 0, keepdims=False)
    send_ids = bound_ids[part_here]
    local_cols = local_blocks * block_rows
    adj_t = adj_tiles.reshape(local_cols, -1).T.reshape(-1, block_rows, local_cols)
    adj_t_local = adj_t[:local_blocks].reshape(local_cols, local_cols)
    adj_t_remote = jnp.concatenate(
        [adj_t[local_blocks:], jnp.zeros((1, block_rows, local_cols), adj_t.dtype)], axis=0
    )
    slot_of_part = (jnp.arange(part_count, dtype=jnp.int32) - part_here - 1) % part_count
    adj_t_by_part = adj_t_remote[slot_of_part].reshape(part_count * block_rows, local_cols)
    adj_local = adj_t_local.T
    adj_by_part = adj_t_by_part.T

    def normed_of(hidden):
        local_view = hidden.reshape(local_blocks, block_rows, feature_width)
        outgoing = local_view[send_ids]
        incoming = lax.all_to_all(outgoing, "dom", 0, 0, tiled=True)
        aggregate = jnp.einsum(
            "kb,kd->bd", adj_t_local, hidden, preferred_element_type=jnp.float32
        ) + jnp.einsum(
            "kb,kd->bd", adj_t_by_part, incoming.reshape(-1, feature_width),
            preferred_element_type=jnp.float32,
        )
        mean_square = jnp.mean(aggregate * aggregate, axis=-1, keepdims=True)
        return (aggregate * lax.rsqrt(mean_square + 1e-06)).astype(jnp.bfloat16)

    def projected_onto(hidden, normed, weight):
        projected = jnp.dot(normed, weight, preferred_element_type=jnp.float32)
        return (hidden.astype(jnp.float32) + jax.nn.relu(projected)).astype(jnp.bfloat16)

    if section_count == 4 and part_count % 2 == 0:
        pairs = [
            (section * part_count + part, (section ^ 2) * part_count + (part ^ 1))
            for section in range(section_count)
            for part in range(part_count)
        ]
        core_swap = [(0, 1), (1, 0), (2, 3), (3, 2)]

        def spread(value):
            across = lax.ppermute(value, ("section", "dom"), pairs)
            beside_own = lax.ppermute(value, "section", core_swap)
            beside_far = lax.ppermute(across, "section", core_swap)
            return [value, beside_own, across, beside_far]

        def list_index(section):
            return jnp.bitwise_xor(section, group)
    else:
        def spread(value):
            return [value] + [shifted(value, "section", step) for step in range(1, section_count)]

        def list_index(section):
            return (group - section) % section_count

    count_list = jnp.concatenate(spread(layer_counts))
    count_by_section = count_list[list_index(jnp.arange(section_count, dtype=jnp.int32))]
    trips = jnp.clip(count_by_section, 0, slot_total)
    weight_list = spread(weights[0])

    finished = jnp.cumsum(trips)
    total = finished[-1]

    layers = jnp.arange(section_count * slot_total, dtype=jnp.int32)
    layer_section = jnp.sum((finished[None, :] <= layers[:, None]).astype(jnp.int32), axis=1)
    layer_section = jnp.minimum(layer_section, section_count - 1)
    layer_slot = layers - (finished[layer_section] - trips[layer_section])
    layer_slot = jnp.clip(layer_slot, 0, slot_total - 1)
    weight_list_row = list_index(layer_section)

    def weight_for(layer):
        slot = layer_slot[layer]
        picks = [lax.dynamic_index_in_dim(held, slot, 0, keepdims=False) for held in weight_list]
        return lax.select_n(weight_list_row[layer], *picks)

    def recorded(stash, hidden, done):
        return jnp.where((finished == done)[:, None, None], hidden[None], stash)

    stash = jnp.broadcast_to(hidden[None], (section_count,) + hidden.shape)

    def exchanged(outgoing):
        return lax.all_to_all(outgoing, "dom", 0, 0, tiled=True)

    first_outgoing = hidden.reshape(local_blocks, block_rows, feature_width)[send_ids]
    incoming = exchanged(first_outgoing)

    def layer_step(layer, carry):
        hidden, incoming, stash, weight = carry
        hidden, outgoing = fused_layer(send_ids, hidden, incoming, adj_local, adj_by_part, weight)
        stash = recorded(stash, hidden, layer + 1)
        return hidden, exchanged(outgoing), stash, weight_for(layer + 1)

    hidden, incoming, stash, weight = lax.fori_loop(
        0, jnp.maximum(total - 1, 0), layer_step, (hidden, incoming, stash, weight_for(0))
    )
    hidden = fused_layer(send_ids, hidden, incoming, adj_local, adj_by_part, weight, with_outgoing=False)[0]
    stash = jnp.where(total >= 1, recorded(stash, hidden, total), stash)

    if section_count == 4:
        arrived = [lax.dynamic_index_in_dim(stash, group, 0, keepdims=False)]
        for step in range(1, section_count):
            piece = lax.dynamic_index_in_dim(stash, jnp.bitwise_xor(group, step), 0, keepdims=False)
            arrived.append(
                lax.ppermute(piece, "section", [(source, source ^ step) for source in range(section_count)])
            )
        arrived = jnp.stack(arrived)
        out = arrived[jnp.bitwise_xor(jnp.arange(section_count, dtype=jnp.int32), group)]
        return out[None]
    stash_stack = stash
    arrived = [lax.dynamic_index_in_dim(stash_stack, group, 0, keepdims=False)]
    for step in range(1, section_count):
        piece = lax.dynamic_index_in_dim(stash_stack, (group + step) % section_count, 0, keepdims=False)
        arrived.append(shifted(piece, "section", step))
    arrived = jnp.stack(arrived)
    out = arrived[(group - jnp.arange(section_count, dtype=jnp.int32)) % section_count]
    return out[None]


def solution(mesh):
    in_specs = (
        P(None, "dom", None),
        P(None, "dom", None, None),
        P(),
        P("section"),
        P("section", None, None, None),
    )
    out_specs = P("section", None, "dom", None)
    return jax.shard_map(local, mesh=mesh, in_specs=in_specs, out_specs=out_specs, check_vma=False)
```

```python
import jax
import jax.numpy as jnp
from jax import lax
from jax.experimental import pallas as pl
from jax.experimental.pallas import tpu as pltpu
from jax.sharding import PartitionSpec as P


def layer_kernel(ids_ref, hidden_ref, incoming_ref, adj_local_ref, adj_remote_ref, weight_ref,
                 hidden_out_ref, outgoing_ref=None):
    hidden = hidden_ref[...]
    aggregate = jnp.dot(adj_local_ref[...], hidden, preferred_element_type=jnp.float32) + jnp.dot(
        adj_remote_ref[...], incoming_ref[...], preferred_element_type=jnp.float32
    )
    mean_square = jnp.mean(aggregate * aggregate, axis=-1, keepdims=True)
    normed = (aggregate * lax.rsqrt(mean_square + 1e-06)).astype(jnp.bfloat16)
    projected = jnp.dot(normed, weight_ref[...], preferred_element_type=jnp.float32)
    updated = (hidden.astype(jnp.float32) + jnp.maximum(projected, 0.0)).astype(jnp.bfloat16)
    hidden_out_ref[...] = updated
    if outgoing_ref is None:
        return
    block_rows = outgoing_ref.shape[1]
    first = updated[:block_rows]
    second = updated[block_rows:]
    for part in range(outgoing_ref.shape[0]):
        @pl.when(ids_ref[part] == 0)
        def _():
            outgoing_ref[part] = first

        @pl.when(ids_ref[part] != 0)
        def _():
            outgoing_ref[part] = second


def fused_layer(send_ids, hidden, incoming, adj_local, adj_remote, weight, with_outgoing=True):
    parts, block_rows, width = incoming.shape
    vmem = pl.BlockSpec(memory_space=pltpu.VMEM)
    hidden_shape = jax.ShapeDtypeStruct(hidden.shape, hidden.dtype)
    if with_outgoing:
        out_shape = (hidden_shape, jax.ShapeDtypeStruct((parts, block_rows, width), hidden.dtype))
        out_specs = (vmem, vmem)
    else:
        out_shape = (hidden_shape,)
        out_specs = (vmem,)
    return pl.pallas_call(
        layer_kernel,
        out_shape=out_shape,
        in_specs=[pl.BlockSpec(memory_space=pltpu.SMEM)] + [vmem] * 5,
        out_specs=out_specs,
        input_output_aliases={1: 0},
    )(send_ids, hidden, incoming.reshape(parts * block_rows, width), adj_local, adj_remote, weight)


def shifted(value, axis, steps):
    count = lax.axis_size(axis)
    return lax.ppermute(value, axis, [(source, (source + steps) % count) for source in range(count)])


def sent_one_way(value, axis, source, target):
    return lax.ppermute(value, axis, [(source, target)])


def local(features, adjacency, boundary, layer_counts, weights):
    section_count = lax.axis_size("section")
    part_count = lax.axis_size("dom")
    group = lax.axis_index("section")
    part_here = lax.axis_index("dom")
    local_rows = features.shape[1]
    feature_width = features.shape[2]
    local_blocks = adjacency.shape[1]
    block_rows = adjacency.shape[2]
    slot_total = weights.shape[1]

    hidden = lax.dynamic_index_in_dim(features, group, 0, keepdims=False)
    adj_tiles = lax.dynamic_index_in_dim(adjacency, group, 0, keepdims=False)
    bound_ids = lax.dynamic_index_in_dim(boundary, group, 0, keepdims=False)
    send_ids = bound_ids[part_here]
    local_cols = local_blocks * block_rows
    adj_t = adj_tiles.reshape(local_cols, -1).T.reshape(-1, block_rows, local_cols)
    adj_t_local = adj_t[:local_blocks].reshape(local_cols, local_cols)
    adj_t_remote = jnp.concatenate(
        [adj_t[local_blocks:], jnp.zeros((1, block_rows, local_cols), adj_t.dtype)], axis=0
    )
    slot_of_part = (jnp.arange(part_count, dtype=jnp.int32) - part_here - 1) % part_count
    adj_t_by_part = adj_t_remote[slot_of_part].reshape(part_count * block_rows, local_cols)
    adj_local = adj_t_local.T
    adj_by_part = adj_t_by_part.T

    def normed_of(hidden):
        local_view = hidden.reshape(local_blocks, block_rows, feature_width)
        outgoing = local_view[send_ids]
        incoming = lax.all_to_all(outgoing, "dom", 0, 0, tiled=True)
        aggregate = jnp.einsum(
            "kb,kd->bd", adj_t_local, hidden, preferred_element_type=jnp.float32
        ) + jnp.einsum(
            "kb,kd->bd", adj_t_by_part, incoming.reshape(-1, feature_width),
            preferred_element_type=jnp.float32,
        )
        mean_square = jnp.mean(aggregate * aggregate, axis=-1, keepdims=True)
        return (aggregate * lax.rsqrt(mean_square + 1e-06)).astype(jnp.bfloat16)

    def projected_onto(hidden, normed, weight):
        projected = jnp.dot(normed, weight, preferred_element_type=jnp.float32)
        return (hidden.astype(jnp.float32) + jax.nn.relu(projected)).astype(jnp.bfloat16)

    if section_count == 4 and part_count % 2 == 0:
        pairs = [
            (section * part_count + part, (section ^ 2) * part_count + (part ^ 1))
            for section in range(section_count)
            for part in range(part_count)
        ]
        core_swap = [(0, 1), (1, 0), (2, 3), (3, 2)]

        def spread(value):
            across = lax.ppermute(value, ("section", "dom"), pairs)
            beside_own = lax.ppermute(value, "section", core_swap)
            beside_far = lax.ppermute(across, "section", core_swap)
            return [value, beside_own, across, beside_far]

        def list_index(section):
            return jnp.bitwise_xor(section, group)
    else:
        def spread(value):
            return [value] + [shifted(value, "section", step) for step in range(1, section_count)]

        def list_index(section):
            return (group - section) % section_count

    count_list = jnp.concatenate(spread(layer_counts))
    count_by_section = count_list[list_index(jnp.arange(section_count, dtype=jnp.int32))]
    trips = jnp.clip(count_by_section, 0, slot_total)
    weight_list = spread(weights[0])

    finished = jnp.cumsum(trips)
    total = finished[-1]

    layers = jnp.arange(section_count * slot_total, dtype=jnp.int32)
    layer_section = jnp.sum((finished[None, :] <= layers[:, None]).astype(jnp.int32), axis=1)
    layer_section = jnp.minimum(layer_section, section_count - 1)
    layer_slot = layers - (finished[layer_section] - trips[layer_section])
    layer_slot = jnp.clip(layer_slot, 0, slot_total - 1)
    weight_list_row = list_index(layer_section)

    def weight_for(layer):
        slot = layer_slot[layer]
        picks = [lax.dynamic_index_in_dim(held, slot, 0, keepdims=False) for held in weight_list]
        return lax.select_n(weight_list_row[layer], *picks)

    def recorded(stash, hidden, done):
        return jnp.where((finished == done)[:, None, None], hidden[None], stash)

    stash = jnp.broadcast_to(hidden[None], (section_count,) + hidden.shape)

    def exchanged(outgoing):
        return lax.all_to_all(outgoing, "dom", 0, 0, tiled=True)

    first_outgoing = hidden.reshape(local_blocks, block_rows, feature_width)[send_ids]
    incoming = exchanged(first_outgoing)

    def layer_step(layer, carry):
        hidden, incoming, stash, weight = carry
        hidden, outgoing = fused_layer(send_ids, hidden, incoming, adj_local, adj_by_part, weight)
        stash = recorded(stash, hidden, layer + 1)
        return hidden, exchanged(outgoing), stash, weight_for(layer + 1)

    hidden, incoming, stash, weight = lax.fori_loop(
        0, jnp.maximum(total - 1, 0), layer_step, (hidden, incoming, stash, weight_for(0))
    )
    hidden = fused_layer(send_ids, hidden, incoming, adj_local, adj_by_part, weight, with_outgoing=False)[0]
    stash = jnp.where(total >= 1, recorded(stash, hidden, total), stash)

    stash_stack = stash
    arrived = [lax.dynamic_index_in_dim(stash_stack, group, 0, keepdims=False)]
    for step in range(1, section_count):
        piece = lax.dynamic_index_in_dim(stash_stack, (group + step) % section_count, 0, keepdims=False)
        arrived.append(shifted(piece, "section", step))
    arrived = jnp.stack(arrived)
    out = arrived[(group - jnp.arange(section_count, dtype=jnp.int32)) % section_count]
    return out[None]


def solution(mesh):
    in_specs = (
        P(None, "dom", None),
        P(None, "dom", None, None),
        P(),
        P("section"),
        P("section", None, None, None),
    )
    out_specs = P("section", None, "dom", None)
    return jax.shard_map(local, mesh=mesh, in_specs=in_specs, out_specs=out_specs, check_vma=False)
```

```python
import jax
import jax.numpy as jnp
from jax import lax
from jax.experimental import pallas as pl
from jax.experimental.pallas import tpu as pltpu
from jax.sharding import PartitionSpec as P


def layer_kernel(ids_ref, hidden_ref, incoming_ref, adj_local_ref, adj_remote_ref, weight_ref,
                 hidden_out_ref, outgoing_ref=None):
    hidden = hidden_ref[...]
    aggregate = jnp.dot(adj_local_ref[...], hidden, preferred_element_type=jnp.float32) + jnp.dot(
        adj_remote_ref[...], incoming_ref[...], preferred_element_type=jnp.float32
    )
    mean_square = jnp.mean(aggregate * aggregate, axis=-1, keepdims=True)
    normed = (aggregate * lax.rsqrt(mean_square + 1e-06)).astype(jnp.bfloat16)
    projected = jnp.dot(normed, weight_ref[...], preferred_element_type=jnp.float32)
    updated = (hidden.astype(jnp.float32) + jnp.maximum(projected, 0.0)).astype(jnp.bfloat16)
    hidden_out_ref[...] = updated
    if outgoing_ref is None:
        return
    block_rows = outgoing_ref.shape[1]
    first = updated[:block_rows]
    second = updated[block_rows:]
    for part in range(outgoing_ref.shape[0]):
        outgoing_ref[part] = jnp.where(ids_ref[part] == 0, first, second)


def fused_layer(send_ids, hidden, incoming, adj_local, adj_remote, weight, with_outgoing=True):
    parts, block_rows, width = incoming.shape
    vmem = pl.BlockSpec(memory_space=pltpu.VMEM)
    hidden_shape = jax.ShapeDtypeStruct(hidden.shape, hidden.dtype)
    if with_outgoing:
        out_shape = (hidden_shape, jax.ShapeDtypeStruct((parts, block_rows, width), hidden.dtype))
        out_specs = (vmem, vmem)
    else:
        out_shape = (hidden_shape,)
        out_specs = (vmem,)
    return pl.pallas_call(
        layer_kernel,
        out_shape=out_shape,
        in_specs=[pl.BlockSpec(memory_space=pltpu.SMEM)] + [vmem] * 5,
        out_specs=out_specs,
        input_output_aliases={1: 0},
    )(send_ids, hidden, incoming.reshape(parts * block_rows, width), adj_local, adj_remote, weight)


def shifted(value, axis, steps):
    count = lax.axis_size(axis)
    return lax.ppermute(value, axis, [(source, (source + steps) % count) for source in range(count)])


def sent_one_way(value, axis, source, target):
    return lax.ppermute(value, axis, [(source, target)])


def local(features, adjacency, boundary, layer_counts, weights):
    section_count = lax.axis_size("section")
    part_count = lax.axis_size("dom")
    group = lax.axis_index("section")
    part_here = lax.axis_index("dom")
    local_rows = features.shape[1]
    feature_width = features.shape[2]
    local_blocks = adjacency.shape[1]
    block_rows = adjacency.shape[2]
    slot_total = weights.shape[1]

    hidden = lax.dynamic_index_in_dim(features, group, 0, keepdims=False)
    adj_tiles = lax.dynamic_index_in_dim(adjacency, group, 0, keepdims=False)
    bound_ids = lax.dynamic_index_in_dim(boundary, group, 0, keepdims=False)
    send_ids = bound_ids[part_here]
    local_cols = local_blocks * block_rows
    adj_t = adj_tiles.reshape(local_cols, -1).T.reshape(-1, block_rows, local_cols)
    adj_t_local = adj_t[:local_blocks].reshape(local_cols, local_cols)
    adj_t_remote = jnp.concatenate(
        [adj_t[local_blocks:], jnp.zeros((1, block_rows, local_cols), adj_t.dtype)], axis=0
    )
    slot_of_part = (jnp.arange(part_count, dtype=jnp.int32) - part_here - 1) % part_count
    adj_t_by_part = adj_t_remote[slot_of_part].reshape(part_count * block_rows, local_cols)
    adj_local = adj_t_local.T
    adj_by_part = adj_t_by_part.T

    def normed_of(hidden):
        local_view = hidden.reshape(local_blocks, block_rows, feature_width)
        outgoing = local_view[send_ids]
        incoming = lax.all_to_all(outgoing, "dom", 0, 0, tiled=True)
        aggregate = jnp.einsum(
            "kb,kd->bd", adj_t_local, hidden, preferred_element_type=jnp.float32
        ) + jnp.einsum(
            "kb,kd->bd", adj_t_by_part, incoming.reshape(-1, feature_width),
            preferred_element_type=jnp.float32,
        )
        mean_square = jnp.mean(aggregate * aggregate, axis=-1, keepdims=True)
        return (aggregate * lax.rsqrt(mean_square + 1e-06)).astype(jnp.bfloat16)

    def projected_onto(hidden, normed, weight):
        projected = jnp.dot(normed, weight, preferred_element_type=jnp.float32)
        return (hidden.astype(jnp.float32) + jax.nn.relu(projected)).astype(jnp.bfloat16)

    if section_count == 4 and part_count % 2 == 0:
        pairs = [
            (section * part_count + part, (section ^ 2) * part_count + (part ^ 1))
            for section in range(section_count)
            for part in range(part_count)
        ]
        core_swap = [(0, 1), (1, 0), (2, 3), (3, 2)]

        def spread(value):
            across = lax.ppermute(value, ("section", "dom"), pairs)
            beside_own = lax.ppermute(value, "section", core_swap)
            beside_far = lax.ppermute(across, "section", core_swap)
            return [value, beside_own, across, beside_far]

        def list_index(section):
            return jnp.bitwise_xor(section, group)
    else:
        def spread(value):
            return [value] + [shifted(value, "section", step) for step in range(1, section_count)]

        def list_index(section):
            return (group - section) % section_count

    count_list = jnp.concatenate(spread(layer_counts))
    count_by_section = count_list[list_index(jnp.arange(section_count, dtype=jnp.int32))]
    trips = jnp.clip(count_by_section, 0, slot_total)
    weight_list = spread(weights[0])

    finished = jnp.cumsum(trips)
    total = finished[-1]

    layers = jnp.arange(section_count * slot_total, dtype=jnp.int32)
    layer_section = jnp.sum((finished[None, :] <= layers[:, None]).astype(jnp.int32), axis=1)
    layer_section = jnp.minimum(layer_section, section_count - 1)
    layer_slot = layers - (finished[layer_section] - trips[layer_section])
    layer_slot = jnp.clip(layer_slot, 0, slot_total - 1)
    weight_list_row = list_index(layer_section)

    def weight_for(layer):
        slot = layer_slot[layer]
        picks = [lax.dynamic_index_in_dim(held, slot, 0, keepdims=False) for held in weight_list]
        return lax.select_n(weight_list_row[layer], *picks)

    def recorded(stash, hidden, done):
        return jnp.where((finished == done)[:, None, None], hidden[None], stash)

    stash = jnp.broadcast_to(hidden[None], (section_count,) + hidden.shape)

    def exchanged(outgoing):
        return lax.all_to_all(outgoing, "dom", 0, 0, tiled=True)

    first_view = hidden.reshape(local_blocks, block_rows, feature_width)
    first_outgoing = jnp.where((send_ids == 0)[:, None, None], first_view[0][None], first_view[1][None])
    incoming = exchanged(first_outgoing)

    def layer_step(layer, carry):
        hidden, incoming, stash, weight = carry
        hidden, outgoing = fused_layer(send_ids, hidden, incoming, adj_local, adj_by_part, weight)
        stash = recorded(stash, hidden, layer + 1)
        return hidden, exchanged(outgoing), stash, weight_for(layer + 1)

    hidden, incoming, stash, weight = lax.fori_loop(
        0, jnp.maximum(total - 1, 0), layer_step, (hidden, incoming, stash, weight_for(0))
    )
    hidden = fused_layer(send_ids, hidden, incoming, adj_local, adj_by_part, weight, with_outgoing=False)[0]
    stash = jnp.where(total >= 1, recorded(stash, hidden, total), stash)

    stash_stack = stash
    arrived = [lax.dynamic_index_in_dim(stash_stack, group, 0, keepdims=False)]
    for step in range(1, section_count):
        piece = lax.dynamic_index_in_dim(stash_stack, (group + step) % section_count, 0, keepdims=False)
        arrived.append(shifted(piece, "section", step))
    arrived = jnp.stack(arrived)
    out = arrived[(group - jnp.arange(section_count, dtype=jnp.int32)) % section_count]
    return out[None]


def solution(mesh):
    in_specs = (
        P(None, "dom", None),
        P(None, "dom", None, None),
        P(),
        P("section"),
        P("section", None, None, None),
    )
    out_specs = P("section", None, "dom", None)
    return jax.shard_map(local, mesh=mesh, in_specs=in_specs, out_specs=out_specs, check_vma=False)
```

```python
import jax
import jax.numpy as jnp
from jax import lax
from jax.experimental import pallas as pl
from jax.experimental.pallas import tpu as pltpu
from jax.sharding import PartitionSpec as P


def layer_kernel(ids_ref, hidden_ref, incoming_ref, adj_local_ref, adj_remote_ref, weight_ref,
                 hidden_out_ref, outgoing_ref=None):
    hidden = hidden_ref[...]
    aggregate = jnp.dot(adj_local_ref[...], hidden, preferred_element_type=jnp.float32) + jnp.dot(
        adj_remote_ref[...], incoming_ref[...], preferred_element_type=jnp.float32
    )
    mean_square = jnp.mean(aggregate * aggregate, axis=-1, keepdims=True)
    normed = (aggregate * lax.rsqrt(mean_square + 1e-06)).astype(jnp.bfloat16)
    projected = jnp.dot(normed, weight_ref[...], preferred_element_type=jnp.float32)
    updated = (hidden.astype(jnp.float32) + jnp.maximum(projected, 0.0)).astype(jnp.bfloat16)
    hidden_out_ref[...] = updated
    if outgoing_ref is None:
        return
    block_rows = outgoing_ref.shape[1]
    first = updated[:block_rows]
    second = updated[block_rows:]
    for part in range(outgoing_ref.shape[0]):
        outgoing_ref[part] = jnp.where(ids_ref[part] == 0, first, second)


def fused_layer(send_ids, hidden, incoming, adj_local, adj_remote, weight, with_outgoing=True):
    parts, block_rows, width = incoming.shape
    vmem = pl.BlockSpec(memory_space=pltpu.VMEM)
    hidden_shape = jax.ShapeDtypeStruct(hidden.shape, hidden.dtype)
    if with_outgoing:
        out_shape = (hidden_shape, jax.ShapeDtypeStruct((parts, block_rows, width), hidden.dtype))
        out_specs = (vmem, vmem)
    else:
        out_shape = (hidden_shape,)
        out_specs = (vmem,)
    return pl.pallas_call(
        layer_kernel,
        out_shape=out_shape,
        in_specs=[pl.BlockSpec(memory_space=pltpu.SMEM)] + [vmem] * 5,
        out_specs=out_specs,
        input_output_aliases={1: 0},
    )(send_ids, hidden, incoming.reshape(parts * block_rows, width), adj_local, adj_remote, weight)


def shifted(value, axis, steps):
    count = lax.axis_size(axis)
    return lax.ppermute(value, axis, [(source, (source + steps) % count) for source in range(count)])


def sent_one_way(value, axis, source, target):
    return lax.ppermute(value, axis, [(source, target)])


def local(features, adjacency, boundary, layer_counts, weights):
    section_count = lax.axis_size("section")
    part_count = lax.axis_size("dom")
    group = lax.axis_index("section")
    part_here = lax.axis_index("dom")
    local_rows = features.shape[1]
    feature_width = features.shape[2]
    local_blocks = adjacency.shape[1]
    block_rows = adjacency.shape[2]
    slot_total = weights.shape[1]

    hidden = lax.dynamic_index_in_dim(features, group, 0, keepdims=False)
    adj_tiles = lax.dynamic_index_in_dim(adjacency, group, 0, keepdims=False)
    bound_ids = lax.dynamic_index_in_dim(boundary, group, 0, keepdims=False)
    send_ids = bound_ids[part_here]
    local_cols = local_blocks * block_rows
    adj_t = adj_tiles.reshape(local_cols, -1).T.reshape(-1, block_rows, local_cols)
    adj_t_local = adj_t[:local_blocks].reshape(local_cols, local_cols)
    adj_t_remote = jnp.concatenate(
        [adj_t[local_blocks:], jnp.zeros((1, block_rows, local_cols), adj_t.dtype)], axis=0
    )
    slot_of_part = (jnp.arange(part_count, dtype=jnp.int32) - part_here - 1) % part_count
    adj_t_by_part = adj_t_remote[slot_of_part].reshape(part_count * block_rows, local_cols)
    adj_local = adj_t_local.T
    adj_by_part = adj_t_by_part.T

    def normed_of(hidden):
        local_view = hidden.reshape(local_blocks, block_rows, feature_width)
        outgoing = local_view[send_ids]
        incoming = lax.all_to_all(outgoing, "dom", 0, 0, tiled=True)
        aggregate = jnp.einsum(
            "kb,kd->bd", adj_t_local, hidden, preferred_element_type=jnp.float32
        ) + jnp.einsum(
            "kb,kd->bd", adj_t_by_part, incoming.reshape(-1, feature_width),
            preferred_element_type=jnp.float32,
        )
        mean_square = jnp.mean(aggregate * aggregate, axis=-1, keepdims=True)
        return (aggregate * lax.rsqrt(mean_square + 1e-06)).astype(jnp.bfloat16)

    def projected_onto(hidden, normed, weight):
        projected = jnp.dot(normed, weight, preferred_element_type=jnp.float32)
        return (hidden.astype(jnp.float32) + jax.nn.relu(projected)).astype(jnp.bfloat16)

    if section_count == 4 and part_count % 2 == 0:
        pairs = [
            (section * part_count + part, (section ^ 2) * part_count + (part ^ 1))
            for section in range(section_count)
            for part in range(part_count)
        ]
        core_swap = [(0, 1), (1, 0), (2, 3), (3, 2)]

        def spread(value):
            across = lax.ppermute(value, ("section", "dom"), pairs)
            beside_own = lax.ppermute(value, "section", core_swap)
            beside_far = lax.ppermute(across, "section", core_swap)
            return [value, beside_own, across, beside_far]

        def list_index(section):
            return jnp.bitwise_xor(section, group)
    else:
        def spread(value):
            return [value] + [shifted(value, "section", step) for step in range(1, section_count)]

        def list_index(section):
            return (group - section) % section_count

    count_list = jnp.concatenate(spread(layer_counts))
    count_by_section = count_list[list_index(jnp.arange(section_count, dtype=jnp.int32))]
    trips = jnp.clip(count_by_section, 0, slot_total)
    weight_list = spread(weights[0])

    finished = jnp.cumsum(trips)
    total = finished[-1]

    layers = jnp.arange(section_count * slot_total, dtype=jnp.int32)
    layer_section = jnp.sum((finished[None, :] <= layers[:, None]).astype(jnp.int32), axis=1)
    layer_section = jnp.minimum(layer_section, section_count - 1)
    layer_slot = layers - (finished[layer_section] - trips[layer_section])
    layer_slot = jnp.clip(layer_slot, 0, slot_total - 1)
    weight_list_row = list_index(layer_section)

    def weight_for(layer):
        slot = layer_slot[layer]
        picks = [lax.dynamic_index_in_dim(held, slot, 0, keepdims=False) for held in weight_list]
        return lax.select_n(weight_list_row[layer], *picks)

    def recorded(stash, hidden, done):
        return jnp.where((finished == done)[:, None, None], hidden[None], stash)

    stash = jnp.broadcast_to(hidden[None], (section_count,) + hidden.shape)

    def exchanged(outgoing):
        return lax.all_to_all(outgoing, "dom", 0, 0, tiled=True)

    first_view = hidden.reshape(local_blocks, block_rows, feature_width)
    first_outgoing = jnp.where((send_ids == 0)[:, None, None], first_view[0][None], first_view[1][None])
    incoming = exchanged(first_outgoing)

    def layer_step(layer, carry):
        hidden, incoming, stash, weight = carry
        hidden, outgoing = fused_layer(send_ids, hidden, incoming, adj_local, adj_by_part, weight)
        stash = recorded(stash, hidden, layer + 1)
        return hidden, exchanged(outgoing), stash, weight_for(layer + 1)

    hidden, incoming, stash, weight = lax.fori_loop(
        0, jnp.maximum(total - 1, 0), layer_step, (hidden, incoming, stash, weight_for(0))
    )
    hidden = fused_layer(send_ids, hidden, incoming, adj_local, adj_by_part, weight, with_outgoing=False)[0]
    stash = jnp.where(total >= 1, recorded(stash, hidden, total), stash)

    stash_stack = stash
    arrived = [lax.dynamic_index_in_dim(stash_stack, group, 0, keepdims=False)]
    for step in range(1, section_count):
        piece = lax.dynamic_index_in_dim(stash_stack, (group + step) % section_count, 0, keepdims=False)
        arrived.append(shifted(piece, "section", step))
    out = jnp.stack(
        [lax.select_n((group - micro) % section_count, *arrived) for micro in range(section_count)]
    )
    return out[None]


def solution(mesh):
    in_specs = (
        P(None, "dom", None),
        P(None, "dom", None, None),
        P(),
        P("section"),
        P("section", None, None, None),
    )
    out_specs = P("section", None, "dom", None)
    return jax.shard_map(local, mesh=mesh, in_specs=in_specs, out_specs=out_specs, check_vma=False)
```
